32 devices in a mesh: dp: 16 (over z, y, x), tensor: 2 (over core).
Axes of the slice: x: 2, y: 2, z: 4, core: 2. Of those that a mesh axis runs over, the one named last changes fastest.
Arguments:
- tokens: bfloat16 [2048, 5120], P('dp', 'tensor'), may hold values from -6 to 6
- cotangent: bfloat16 [2048, 5120], P('dp', 'tensor'), may hold values from -6 to 6
- w_gate: bfloat16 [2, 27, 5, 128, 128], P('tensor'), may hold values from -0.25 to 0.25
- w_up: bfloat16 [2, 27, 5, 128, 128], P('tensor'), may hold values from -0.25 to 0.25
- w_down: bfloat16 [2, 27, 5, 128, 128], P('tensor'), may hold values from -0.25 to 0.25
- col_index: int32 [54, 5], P('tensor'), may hold values from 0 to 39, as said below
- row_count: int32 [54], P('tensor'), may hold values from 2 to 5, as said below
- adam_m: float32 [3, 2, 17280, 128], P(None, 'tensor', 'dp'), may hold values from -4 to 4
- adam_v: float32 [3, 2, 17280, 128], P(None, 'tensor', 'dp'), may hold values from 0.02 to 0.5
Outputs:
- token_grads: bfloat16 [2048, 5120], P('dp', 'tensor')
- first_moment: float32 [3, 2, 17280, 128], P(None, 'tensor', 'dp')
- second_moment: float32 [3, 2, 17280, 128], P(None, 'tensor', 'dp')
- update_dir: float32 [3, 2, 17280, 128], P(None, 'tensor', 'dp')
The draws below stay inside these ranges and needn't reach their ends.
Inputs may be any that keep to these rules, and one draw needn't show every extreme that they name: `col_index`: in each row the first row_count entries are distinct width blocks. `row_count`: some hidden block has exactly 5 live slots.
All inputs are finite; a program needn't handle non-finite values.
Results may differ from the reference program's by a relative error of at most 0.0085.
Values may be sent and summed in bfloat16 or wider, within the bound.
No kernel may reach another device: no remote copies, remote signals or barrier semaphores. Data moves between devices by JAX's collectives and lax.ppermute only.
A program may use at most 192 MiB of HBM per device.

```python
import math
import jax
import jax.numpy as jnp
from jax import lax

D = 5120
BLK = 128
PER_H = 5
TOK_DEV = 128
DBLK = 40
FBLK = 54
HBLK = 27
TOKENS = 2048
N_DP = 16
N_TENSOR = 2


def draw_col_index(key, part):
    row_keys = jax.random.split(key, FBLK)
    orders = jax.vmap(lambda row_key: jax.random.permutation(row_key, DBLK))(row_keys)
    return orders[:, :PER_H].astype(jnp.int32)


def draw_row_count(key, part):
    key_heavy, key_high, key_low, key_pick = jax.random.split(key, 4)
    heavy_shard = jax.random.randint(key_heavy, (), 0, FBLK // HBLK)
    shard_of = jnp.arange(FBLK) // HBLK
    high_counts = jax.random.randint(key_high, (FBLK,), PER_H - 1, PER_H + 1)
    low_counts = jax.random.randint(key_low, (FBLK,), 2, PER_H)
    counts = jnp.where(shard_of == heavy_shard, high_counts, low_counts)
    pick_row = jax.random.randint(key_pick, (), 0, HBLK) + heavy_shard * HBLK
    counts = jnp.where(jnp.arange(FBLK) == pick_row, PER_H, counts)
    return counts.astype(jnp.int32)


def block_levels(rng, shape, cuts, low, largest):
    loudness, own = 1.0, jax.random.fold_in(rng, 6)
    for position, blocks in cuts:
        heights = jnp.exp(jax.random.uniform(jax.random.fold_in(own, position), (blocks,), jnp.float32, low / len(cuts), largest / len(cuts)))
        loudness = loudness * jnp.repeat(heights, shape[position] // blocks).reshape([-1 if axis == position else 1 for axis in range(len(shape))])
    return loudness


def noise(rng, dims, width, bound, cuts=(), held_as=jnp.bfloat16):
    array = width * jax.random.normal(rng, dims, jnp.float32)
    if cuts:
        array = array * block_levels(rng, dims, cuts, -0.22, 0.18)
    return jnp.clip(array, -bound, bound).astype(held_as)


def setup_inputs(seed: int = 0) -> dict:
    keys = jax.random.split(jax.random.key(seed), 10)
    tokens = noise(keys[0], (TOKENS, D), 1.0, 6.0, ((0, 16), (1, 2)))
    cotangent = noise(keys[1], (TOKENS, D), 1.0, 6.0, ((0, 16), (1, 2)))
    w_gate = noise(keys[2], (N_TENSOR, HBLK, PER_H, BLK, BLK), (BLK * PER_H) ** -0.5, 0.25, ((0, 2),))
    w_up = noise(keys[3], (N_TENSOR, HBLK, PER_H, BLK, BLK), (BLK * PER_H) ** -0.5, 0.25, ((0, 2),))
    w_down = noise(keys[4], (N_TENSOR, HBLK, PER_H, BLK, BLK), (BLK * PER_H) ** -0.5, 0.25, ((0, 2),))
    col_index = draw_col_index(jax.random.fold_in(keys[9], 71), 0)
    row_count = draw_row_count(jax.random.fold_in(keys[9], 71), 0)
    adam_m = noise(keys[7], (3, N_TENSOR, HBLK * PER_H * BLK, BLK), 0.3, 4.0, ((1, 2), (2, 16)), jnp.float32)
    adam_v = jnp.clip(jnp.exp(math.log(0.5) - 3.218876 * jax.random.uniform(keys[8], (3, N_TENSOR, HBLK * PER_H * BLK, BLK), jnp.float32) ** block_levels(keys[8], (3, N_TENSOR, HBLK * PER_H * BLK, BLK), ((1, 2), (2, 16)), -0.2, 0.2)), 0.02, 0.5)
    return {"tokens": tokens, "cotangent": cotangent, "w_gate": w_gate, "w_up": w_up, "w_down": w_down, "col_index": col_index, "row_count": row_count, "adam_m": adam_m, "adam_v": adam_v}


def slot_terms(tok_block, cot_block, gate_w, up_w, down_w, columns, counts):
    tok_rows = tok_block.shape[0]
    live_mask = jnp.arange(PER_H)[None, :] < counts[:, None]
    keep_bf = live_mask.astype(jnp.bfloat16)[:, :, None, None]
    gate_eff = (gate_w * keep_bf).astype(jnp.float32)
    up_eff = (up_w * keep_bf).astype(jnp.float32)
    down_eff = (down_w * keep_bf).astype(jnp.float32)
    x_blocks = tok_block.reshape(tok_rows, DBLK, BLK)[:, columns].astype(jnp.float32)
    dy_blocks = cot_block.reshape(tok_rows, DBLK, BLK)[:, columns].astype(jnp.float32)
    gate_act = jnp.einsum('thpk,hpkj->thj', x_blocks, gate_eff)
    up_act = jnp.einsum('thpk,hpkj->thj', x_blocks, up_eff)
    sig_gate = jax.nn.sigmoid(gate_act)
    silu_gate = gate_act * sig_gate
    hidden = (silu_gate * up_act).astype(jnp.bfloat16)
    d_hidden = jnp.einsum('thpk,hpjk->thj', dy_blocks, down_eff)
    d_gate = (d_hidden * up_act * sig_gate * (1.0 + gate_act * (1.0 - sig_gate))).astype(jnp.bfloat16)
    d_up = (d_hidden * silu_gate).astype(jnp.bfloat16)
    live_f = live_mask.astype(jnp.float32)[:, :, None, None]
    grad_down = jnp.einsum('thj,thpk->hpjk', hidden.astype(jnp.float32), dy_blocks) * live_f
    grad_gate = jnp.einsum('thpk,thj->hpkj', x_blocks, d_gate.astype(jnp.float32)) * live_f
    grad_up = jnp.einsum('thpk,thj->hpkj', x_blocks, d_up.astype(jnp.float32)) * live_f
    back_term = jnp.einsum('thj,hpkj->thpk', d_gate.astype(jnp.float32), gate_eff)
    back_term = back_term + jnp.einsum('thj,hpkj->thpk', d_up.astype(jnp.float32), up_eff)
    onehot = (columns[:, :, None] == jnp.arange(DBLK)[None, None, :]).astype(jnp.float32)
    dx_piece = jnp.einsum('thpk,hpd->tdk', back_term, onehot, precision=lax.Precision.HIGHEST)
    return (dx_piece.reshape(tok_rows, D), jnp.stack([grad_gate, grad_up, grad_down]))

def reference(tokens, cotangent, w_gate, w_up, w_down, col_index, row_count, adam_m, adam_v):
    columns = col_index.reshape(N_TENSOR, HBLK, PER_H)
    counts = row_count.reshape(N_TENSOR, HBLK)
    tok_groups = tokens.reshape(N_DP, TOK_DEV, D)
    cot_groups = cotangent.reshape(N_DP, TOK_DEV, D)

    def scan_step(running, token_pair):
        tok_block, cot_block = token_pair
        dx_total = jnp.zeros((TOK_DEV, D), jnp.float32)
        grad_list = []
        for shard_idx in range(N_TENSOR):
            dx_piece, grad_piece = slot_terms(tok_block, cot_block, w_gate[shard_idx], w_up[shard_idx], w_down[shard_idx], columns[shard_idx], counts[shard_idx])
            dx_total = dx_total + dx_piece
            grad_list.append(grad_piece)
        return (running + jnp.stack(grad_list), dx_total.astype(jnp.bfloat16))
    start_sum = jnp.zeros((N_TENSOR, 3, HBLK, PER_H, BLK, BLK), jnp.float32)
    grad_total, dx_all = lax.scan(scan_step, start_sum, (tok_groups, cot_groups))
    grad_scale = 1.0 / math.sqrt(TOKENS)
    grad_all = jnp.transpose(grad_total, (1, 0, 2, 3, 4, 5)).reshape(3, N_TENSOR, HBLK * PER_H * BLK, BLK) * grad_scale
    m_new = 0.9 * adam_m + 0.1 * grad_all
    v_new = 0.95 * adam_v + 0.05 * grad_all * grad_all
    step_dir = m_new / (jnp.sqrt(v_new) + 1e-08)
    return (dx_all.reshape(TOKENS, D), m_new, v_new, step_dir)
```

```python
import functools
import math

import jax
import jax.numpy as jnp
from jax import lax
from jax.sharding import PartitionSpec as P

D = 5120
BLK = 128


def ring_order(n):
    if n != 16:
        return list(range(n))
    plane = [(0, 0), (1, 0), (1, 1), (0, 1)]
    order = []
    for q, (x, y) in enumerate(plane):
        zs = range(4) if q % 2 == 0 else range(3, -1, -1)
        order += [z * 4 + y * 2 + x for z in zs]
    return order


def ring_reduce_scatter(full, n, nt, order, wire_dtype):
    chunk = full.shape[1] // n
    pos_of = [0] * n
    for p, d in enumerate(order):
        pos_of[d] = p
    me = jnp.asarray(pos_of, jnp.int32)[lax.axis_index("dp")]
    step = 1 - 2 * (lax.axis_index("tensor") % 2)
    order_arr = jnp.asarray(order, jnp.int32)

    def own(s):
        p = (me - step * (1 + s)) % n
        return lax.dynamic_slice_in_dim(full, order_arr[p] * chunk, chunk, axis=1)

    perm = []
    for p in range(n):
        for t in range(nt):
            hop = 1 if t % 2 == 0 else -1
            perm.append((order[p] * nt + t, order[(p + hop) % n] * nt + t))
    acc = own(0)
    for s in range(1, n):
        moved = lax.ppermute(acc.astype(wire_dtype), ("dp", "tensor"), perm)
        acc = moved.astype(jnp.float32) + own(s)
    return acc


def shards(n_dp, n_t, tokens, cotangent, w_gate, w_up, w_down, col_index, row_count, adam_m, adam_v):
    full_tok, full_cot = (
        lax.all_gather(tokens, "tensor", axis=1, tiled=True),
        lax.all_gather(cotangent, "tensor", axis=1, tiled=True),
    )
    tok_rows = full_tok.shape[0]
    gate_w = w_gate[0]
    up_w = w_up[0]
    down_w = w_down[0]
    slot_count = gate_w.shape[1]
    own_rows = gate_w.shape[0] * slot_count * BLK
    live_mask = jnp.arange(slot_count)[None, :] < row_count[:, None]
    keep_bf = live_mask.astype(jnp.bfloat16)[:, :, None, None]
    gate_eff = gate_w * keep_bf
    up_eff = up_w * keep_bf
    down_eff = down_w * keep_bf
    x_blocks = full_tok.reshape(tok_rows, D // BLK, BLK)[:, col_index]
    dy_blocks = full_cot.reshape(tok_rows, D // BLK, BLK)[:, col_index]
    gate_act = jnp.einsum("thpk,hpkj->thj", x_blocks, gate_eff, preferred_element_type=jnp.float32)
    up_act = jnp.einsum("thpk,hpkj->thj", x_blocks, up_eff, preferred_element_type=jnp.float32)
    sig_gate = jax.nn.sigmoid(gate_act)
    silu_gate = gate_act * sig_gate
    hidden = (silu_gate * up_act).astype(jnp.bfloat16)
    d_hidden = jnp.einsum("thpk,hpjk->thj", dy_blocks, down_eff, preferred_element_type=jnp.float32)
    live_f = live_mask.astype(jnp.float32)[:, :, None, None]
    grad_down = (
        jnp.einsum("thj,thpk->hpjk", hidden, dy_blocks, preferred_element_type=jnp.float32) * live_f
    )
    d_gate = (d_hidden * up_act * sig_gate * (1.0 + gate_act * (1.0 - sig_gate))).astype(
        jnp.bfloat16
    )
    d_up = (d_hidden * silu_gate).astype(jnp.bfloat16)
    grad_gate = (
        jnp.einsum("thpk,thj->hpkj", x_blocks, d_gate, preferred_element_type=jnp.float32) * live_f
    )
    grad_up = (
        jnp.einsum("thpk,thj->hpkj", x_blocks, d_up, preferred_element_type=jnp.float32) * live_f
    )
    back_term = jnp.einsum("thj,hpkj->thpk", d_gate, gate_eff, preferred_element_type=jnp.float32)
    back_term = back_term + jnp.einsum(
        "thj,hpkj->thpk", d_up, up_eff, preferred_element_type=jnp.float32
    )
    onehot = (col_index[:, :, None] == jnp.arange(D // BLK)[None, None, :]).astype(jnp.float32)
    dx_blocks = jnp.einsum("thpk,hpd->tdk", back_term, onehot, precision=lax.Precision.HIGHEST)
    dx_part = dx_blocks.reshape(tok_rows, D)
    reduced = ring_reduce_scatter(
        jnp.stack([grad_gate, grad_up, grad_down]).reshape(3, own_rows, BLK),
        n_dp,
        n_t,
        ring_order(n_dp),
        jnp.float32,
    )[:, None]
    token_grads = lax.psum_scatter(
        dx_part.astype(jnp.bfloat16), "tensor", scatter_dimension=1, tiled=True
    )
    grad_scale = 1.0 / math.sqrt(n_dp * tok_rows)
    grad_all = reduced * grad_scale
    m_new = 0.9 * adam_m + 0.1 * grad_all
    v_new = 0.95 * adam_v + 0.05 * grad_all * grad_all
    step_dir = m_new / (jnp.sqrt(v_new) + 1e-08)
    return (token_grads, m_new, v_new, step_dir)


def solution(mesh):
    in_specs = (
        P("dp", "tensor"),
        P("dp", "tensor"),
        P("tensor", None, None, None, None),
        P("tensor", None, None, None, None),
        P("tensor", None, None, None, None),
        P("tensor", None),
        P("tensor"),
        P(None, "tensor", "dp", None),
        P(None, "tensor", "dp", None),
    )
    out_specs = (
        P("dp", "tensor"),
        P(None, "tensor", "dp", None),
        P(None, "tensor", "dp", None),
        P(None, "tensor", "dp", None),
    )
    body = functools.partial(shards, mesh.shape["dp"], mesh.shape["tensor"])
    return jax.shard_map(body, mesh=mesh, in_specs=in_specs, out_specs=out_specs, check_vma=False)
```

```python
import functools
import math

import jax
import jax.numpy as jnp
from jax import lax
from jax.sharding import PartitionSpec as P

D = 5120
BLK = 128


def ring_order(n):
    if n != 16:
        return list(range(n))
    plane = [(0, 0), (1, 0), (1, 1), (0, 1)]
    order = []
    for q, (x, y) in enumerate(plane):
        zs = range(4) if q % 2 == 0 else range(3, -1, -1)
        order += [z * 4 + y * 2 + x for z in zs]
    return order


def ring_reduce_scatter(streams, n, nt, order, wire_dtype):
    chunk = streams[0].shape[0] // n
    pos_of = [0] * n
    for p, d in enumerate(order):
        pos_of[d] = p
    me = jnp.asarray(pos_of, jnp.int32)[lax.axis_index("dp")]
    step = 1 - 2 * (lax.axis_index("tensor") % 2)
    order_arr = jnp.asarray(order, jnp.int32)

    def own(full, s):
        p = (me - step * (1 + s)) % n
        return lax.dynamic_slice_in_dim(full, order_arr[p] * chunk, chunk, axis=0)

    perm = []
    for p in range(n):
        for t in range(nt):
            hop = 1 if t % 2 == 0 else -1
            perm.append((order[p] * nt + t, order[(p + hop) % n] * nt + t))
    accs = [own(full, 0) for full in streams]
    for s in range(1, n):
        for i, full in enumerate(streams):
            moved = lax.ppermute(accs[i].astype(wire_dtype), ("dp", "tensor"), perm)
            accs[i] = moved.astype(jnp.float32) + own(full, s)
    return accs


def shards(n_dp, n_t, tokens, cotangent, w_gate, w_up, w_down, col_index, row_count, adam_m, adam_v):
    full_tok, full_cot = (
        lax.all_gather(tokens, "tensor", axis=1, tiled=True),
        lax.all_gather(cotangent, "tensor", axis=1, tiled=True),
    )
    tok_rows = full_tok.shape[0]
    gate_w = w_gate[0]
    up_w = w_up[0]
    down_w = w_down[0]
    slot_count = gate_w.shape[1]
    own_rows = gate_w.shape[0] * slot_count * BLK
    live_mask = jnp.arange(slot_count)[None, :] < row_count[:, None]
    keep_bf = live_mask.astype(jnp.bfloat16)[:, :, None, None]
    gate_eff = gate_w * keep_bf
    up_eff = up_w * keep_bf
    down_eff = down_w * keep_bf
    x_blocks = full_tok.reshape(tok_rows, D // BLK, BLK)[:, col_index]
    dy_blocks = full_cot.reshape(tok_rows, D // BLK, BLK)[:, col_index]
    gate_act = jnp.einsum("thpk,hpkj->thj", x_blocks, gate_eff, preferred_element_type=jnp.float32)
    up_act = jnp.einsum("thpk,hpkj->thj", x_blocks, up_eff, preferred_element_type=jnp.float32)
    sig_gate = jax.nn.sigmoid(gate_act)
    silu_gate = gate_act * sig_gate
    hidden = (silu_gate * up_act).astype(jnp.bfloat16)
    d_hidden = jnp.einsum("thpk,hpjk->thj", dy_blocks, down_eff, preferred_element_type=jnp.float32)
    live_f = live_mask.astype(jnp.float32)[:, :, None, None]
    grad_down = (
        jnp.einsum("thj,thpk->hpjk", hidden, dy_blocks, preferred_element_type=jnp.float32) * live_f
    )
    d_gate = (d_hidden * up_act * sig_gate * (1.0 + gate_act * (1.0 - sig_gate))).astype(
        jnp.bfloat16
    )
    d_up = (d_hidden * silu_gate).astype(jnp.bfloat16)
    grad_gate = (
        jnp.einsum("thpk,thj->hpkj", x_blocks, d_gate, preferred_element_type=jnp.float32) * live_f
    )
    grad_up = (
        jnp.einsum("thpk,thj->hpkj", x_blocks, d_up, preferred_element_type=jnp.float32) * live_f
    )
    back_term = jnp.einsum("thj,hpkj->thpk", d_gate, gate_eff, preferred_element_type=jnp.float32)
    back_term = back_term + jnp.einsum(
        "thj,hpkj->thpk", d_up, up_eff, preferred_element_type=jnp.float32
    )
    onehot = (col_index[:, :, None] == jnp.arange(D // BLK)[None, None, :]).astype(jnp.float32)
    dx_blocks = jnp.einsum("thpk,hpd->tdk", back_term, onehot, precision=lax.Precision.HIGHEST)
    dx_part = dx_blocks.reshape(tok_rows, D)
    reduced = jnp.stack(
        ring_reduce_scatter(
            [g.reshape(own_rows, BLK) for g in (grad_gate, grad_up, grad_down)],
            n_dp,
            n_t,
            ring_order(n_dp),
            jnp.bfloat16,
        )
    )[:, None]
    token_grads = lax.psum_scatter(
        dx_part.astype(jnp.bfloat16), "tensor", scatter_dimension=1, tiled=True
    )
    grad_scale = 1.0 / math.sqrt(n_dp * tok_rows)
    grad_all = reduced * grad_scale
    m_new = 0.9 * adam_m + 0.1 * grad_all
    v_new = 0.95 * adam_v + 0.05 * grad_all * grad_all
    step_dir = m_new / (jnp.sqrt(v_new) + 1e-08)
    return (token_grads, m_new, v_new, step_dir)


def solution(mesh):
    in_specs = (
        P("dp", "tensor"),
        P("dp", "tensor"),
        P("tensor", None, None, None, None),
        P("tensor", None, None, None, None),
        P("tensor", None, None, None, None),
        P("tensor", None),
        P("tensor"),
        P(None, "tensor", "dp", None),
        P(None, "tensor", "dp", None),
    )
    out_specs = (
        P("dp", "tensor"),
        P(None, "tensor", "dp", None),
        P(None, "tensor", "dp", None),
        P(None, "tensor", "dp", None),
    )
    body = functools.partial(shards, mesh.shape["dp"], mesh.shape["tensor"])
    return jax.shard_map(body, mesh=mesh, in_specs=in_specs, out_specs=out_specs, check_vma=False)
```

```python
import functools
import math

import jax
import jax.numpy as jnp
from jax import lax
from jax.experimental import pallas as pl
from jax.experimental.pallas import tpu as pltpu
from jax.sharding import PartitionSpec as P

D = 5120
BLK = 128


def ring_order(n):
    if n != 16:
        return list(range(n))
    plane = [(0, 0), (1, 0), (1, 1), (0, 1)]
    order = []
    for q, (x, y) in enumerate(plane):
        zs = range(4) if q % 2 == 0 else range(3, -1, -1)
        order += [z * 4 + y * 2 + x for z in zs]
    return order


def ring_reduce_scatter(streams, n, nt, order, wire_dtype):
    chunk = streams[0].shape[0] // n
    pos_of = [0] * n
    for p, d in enumerate(order):
        pos_of[d] = p
    me = jnp.asarray(pos_of, jnp.int32)[lax.axis_index("dp")]
    step = 1 - 2 * (lax.axis_index("tensor") % 2)
    order_arr = jnp.asarray(order, jnp.int32)

    def own(full, s):
        p = (me - step * (1 + s)) % n
        return lax.dynamic_slice_in_dim(full, order_arr[p] * chunk, chunk, axis=0)

    perm = []
    for p in range(n):
        for t in range(nt):
            hop = 1 if t % 2 == 0 else -1
            perm.append((order[p] * nt + t, order[(p + hop) % n] * nt + t))
    accs = [own(full, 0) for full in streams]
    for s in range(1, n):
        for i, full in enumerate(streams):
            moved = lax.ppermute(accs[i].astype(wire_dtype), ("dp", "tensor"), perm)
            accs[i] = moved.astype(jnp.float32) + own(full, s)
    return accs


def _ffn_kernel(col_ref, cnt_ref, tok_ref, cot_ref, wg_ref, wu_ref, wd_ref,
                gg_ref, gu_ref, gd_ref, dx_ref):
    h = pl.program_id(0)
    slots = wg_ref.shape[1]
    count = cnt_ref[h]

    @pl.when(h == 0)
    def _():
        dx_ref[...] = jnp.zeros_like(dx_ref)

    offs, xs, dys, wgs, wus, wds = [], [], [], [], [], []
    for p in range(slots):
        off = pl.multiple_of(col_ref[h, p] * BLK, BLK)
        live = p < count
        offs.append(off)
        xs.append(tok_ref[:, pl.ds(off, BLK)])
        dys.append(cot_ref[:, pl.ds(off, BLK)])
        wgs.append(jnp.where(live, wg_ref[0, p], jnp.zeros_like(wg_ref[0, p])))
        wus.append(jnp.where(live, wu_ref[0, p], jnp.zeros_like(wu_ref[0, p])))
        wds.append(jnp.where(live, wd_ref[0, p], jnp.zeros_like(wd_ref[0, p])))
    f32 = jnp.float32
    nt = (((1,), (1,)), ((), ()))
    tn = (((0,), (0,)), ((), ()))
    gate = sum(jnp.dot(xs[p], wgs[p], preferred_element_type=f32) for p in range(slots))
    up = sum(jnp.dot(xs[p], wus[p], preferred_element_type=f32) for p in range(slots))
    d_hidden = sum(
        lax.dot_general(dys[p], wds[p], nt, preferred_element_type=f32) for p in range(slots)
    )
    sig = 1.0 / (1.0 + jnp.exp(-gate))
    silu = gate * sig
    hidden = (silu * up).astype(jnp.bfloat16)
    d_gate = (d_hidden * up * sig * (1.0 + gate * (1.0 - sig))).astype(jnp.bfloat16)
    d_up = (d_hidden * silu).astype(jnp.bfloat16)
    for p in range(slots):
        live = p < count
        zero = jnp.zeros((BLK, BLK), f32)
        gg = lax.dot_general(xs[p], d_gate, tn, preferred_element_type=f32)
        gu = lax.dot_general(xs[p], d_up, tn, preferred_element_type=f32)
        gd = lax.dot_general(hidden, dys[p], tn, preferred_element_type=f32)
        gg_ref[0, p] = jnp.where(live, gg, zero)
        gu_ref[0, p] = jnp.where(live, gu, zero)
        gd_ref[0, p] = jnp.where(live, gd, zero)
        back = lax.dot_general(d_gate, wgs[p], nt, preferred_element_type=f32)
        back = back + lax.dot_general(d_up, wus[p], nt, preferred_element_type=f32)
        dx_ref[:, pl.ds(offs[p], BLK)] += back


def ffn_block_terms(col_index, row_count, full_tok, full_cot, gate_w, up_w, down_w):
    hblk, slots = col_index.shape
    rows, width = full_tok.shape
    wspec = pl.BlockSpec((1, slots, BLK, BLK), lambda h, c, n: (h, 0, 0, 0))
    full = pl.BlockSpec((rows, width), lambda h, c, n: (0, 0))
    grad = jax.ShapeDtypeStruct((hblk, slots, BLK, BLK), jnp.float32)
    flops = 2 * rows * hblk * slots * BLK * BLK * 9
    return pl.pallas_call(
        _ffn_kernel,
        grid_spec=pltpu.PrefetchScalarGridSpec(
            num_scalar_prefetch=2,
            grid=(hblk,),
            in_specs=[full, full, wspec, wspec, wspec],
            out_specs=[wspec, wspec, wspec, full],
        ),
        out_shape=[grad, grad, grad, jax.ShapeDtypeStruct((rows, width), jnp.float32)],
        compiler_params=pltpu.CompilerParams(dimension_semantics=("arbitrary",)),
        cost_estimate=pl.CostEstimate(
            flops=flops,
            transcendentals=rows * hblk * BLK,
            bytes_accessed=3 * hblk * slots * BLK * BLK * 6 + rows * width * 8,
        ),
        name="ffn_block_terms",
    )(col_index, row_count, full_tok, full_cot, gate_w, up_w, down_w)


def shards(n_dp, n_t, tokens, cotangent, w_gate, w_up, w_down, col_index, row_count, adam_m, adam_v):
    full_tok, full_cot = (
        lax.all_gather(tokens, "tensor", axis=1, tiled=True),
        lax.all_gather(cotangent, "tensor", axis=1, tiled=True),
    )
    tok_rows = full_tok.shape[0]
    own_rows = w_gate.shape[1] * w_gate.shape[2] * BLK
    grad_gate, grad_up, grad_down, dx_part = ffn_block_terms(
        col_index, row_count, full_tok, full_cot, w_gate[0], w_up[0], w_down[0]
    )
    reduced = jnp.stack(
        ring_reduce_scatter(
            [g.reshape(own_rows, BLK) for g in (grad_gate, grad_up, grad_down)],
            n_dp,
            n_t,
            ring_order(n_dp),
            jnp.bfloat16,
        )
    )[:, None]
    token_grads = lax.psum_scatter(
        dx_part.astype(jnp.bfloat16), "tensor", scatter_dimension=1, tiled=True
    )
    grad_scale = 1.0 / math.sqrt(n_dp * tok_rows)
    grad_all = reduced * grad_scale
    m_new = 0.9 * adam_m + 0.1 * grad_all
    v_new = 0.95 * adam_v + 0.05 * grad_all * grad_all
    step_dir = m_new / (jnp.sqrt(v_new) + 1e-08)
    return (token_grads, m_new, v_new, step_dir)


def solution(mesh):
    in_specs = (
        P("dp", "tensor"),
        P("dp", "tensor"),
        P("tensor", None, None, None, None),
        P("tensor", None, None, None, None),
        P("tensor", None, None, None, None),
        P("tensor", None),
        P("tensor"),
        P(None, "tensor", "dp", None),
        P(None, "tensor", "dp", None),
    )
    out_specs = (
        P("dp", "tensor"),
        P(None, "tensor", "dp", None),
        P(None, "tensor", "dp", None),
        P(None, "tensor", "dp", None),
    )
    body = functools.partial(shards, mesh.shape["dp"], mesh.shape["tensor"])
    return jax.shard_map(body, mesh=mesh, in_specs=in_specs, out_specs=out_specs, check_vma=False)
```

```python
import functools
import math

import jax
import jax.numpy as jnp
from jax import lax
from jax.experimental import pallas as pl
from jax.experimental.pallas import tpu as pltpu
from jax.sharding import PartitionSpec as P

D = 5120
BLK = 128


def ring_order(n):
    if n != 16:
        return list(range(n))
    plane = [(0, 0), (1, 0), (1, 1), (0, 1)]
    order = []
    for q, (x, y) in enumerate(plane):
        zs = range(4) if q % 2 == 0 else range(3, -1, -1)
        order += [z * 4 + y * 2 + x for z in zs]
    return order


def ring_reduce_scatter(streams, n, nt, order, wire_dtype):
    chunk = streams[0].shape[0] // n
    pos_of = [0] * n
    for p, d in enumerate(order):
        pos_of[d] = p
    me = jnp.asarray(pos_of, jnp.int32)[lax.axis_index("dp")]
    step = 1 - 2 * (lax.axis_index("tensor") % 2)
    order_arr = jnp.asarray(order, jnp.int32)

    def own(full, s):
        p = (me - step * (1 + s)) % n
        return lax.dynamic_slice_in_dim(full, order_arr[p] * chunk, chunk, axis=0)

    perm = []
    for p in range(n):
        for t in range(nt):
            hop = 1 if t % 2 == 0 else -1
            perm.append((order[p] * nt + t, order[(p + hop) % n] * nt + t))
    accs = [own(full, 0) for full in streams]
    for s in range(1, n):
        for i, full in enumerate(streams):
            moved = lax.ppermute(accs[i].astype(wire_dtype), ("dp", "tensor"), perm)
            accs[i] = moved.astype(jnp.float32) + own(full, s)
    return accs


def _ffn_kernel(col_ref, cnt_ref, tok_ref, cot_ref, wg_ref, wu_ref, wd_ref,
                gg_ref, gu_ref, gd_ref, dx_ref):
    h = pl.program_id(0)
    slots = wg_ref.shape[1]
    count = cnt_ref[h]

    @pl.when(h == 0)
    def _():
        dx_ref[...] = jnp.zeros_like(dx_ref)

    offs, xs, dys, wgs, wus, wds = [], [], [], [], [], []
    for p in range(slots):
        off = pl.multiple_of(col_ref[h, p] * BLK, BLK)
        live = p < count
        offs.append(off)
        xs.append(tok_ref[:, pl.ds(off, BLK)])
        dys.append(cot_ref[:, pl.ds(off, BLK)])
        wgs.append(jnp.where(live, wg_ref[0, p], jnp.zeros_like(wg_ref[0, p])))
        wus.append(jnp.where(live, wu_ref[0, p], jnp.zeros_like(wu_ref[0, p])))
        wds.append(jnp.where(live, wd_ref[0, p], jnp.zeros_like(wd_ref[0, p])))
    f32 = jnp.float32
    nt = (((1,), (1,)), ((), ()))
    tn = (((0,), (0,)), ((), ()))
    gate = sum(jnp.dot(xs[p], wgs[p], preferred_element_type=f32) for p in range(slots))
    up = sum(jnp.dot(xs[p], wus[p], preferred_element_type=f32) for p in range(slots))
    d_hidden = sum(
        lax.dot_general(dys[p], wds[p], nt, preferred_element_type=f32) for p in range(slots)
    )
    sig = 1.0 / (1.0 + jnp.exp(-gate))
    silu = gate * sig
    hidden = (silu * up).astype(jnp.bfloat16)
    d_gate = (d_hidden * up * sig * (1.0 + gate * (1.0 - sig))).astype(jnp.bfloat16)
    d_up = (d_hidden * silu).astype(jnp.bfloat16)
    for p in range(slots):
        live = p < count
        zero = jnp.zeros((BLK, BLK), f32)
        gg = lax.dot_general(xs[p], d_gate, tn, preferred_element_type=f32)
        gu = lax.dot_general(xs[p], d_up, tn, preferred_element_type=f32)
        gd = lax.dot_general(hidden, dys[p], tn, preferred_element_type=f32)
        gg_ref[0, p] = jnp.where(live, gg, zero)
        gu_ref[0, p] = jnp.where(live, gu, zero)
        gd_ref[0, p] = jnp.where(live, gd, zero)
        back = lax.dot_general(d_gate, wgs[p], nt, preferred_element_type=f32)
        back = back + lax.dot_general(d_up, wus[p], nt, preferred_element_type=f32)
        dx_ref[:, pl.ds(offs[p], BLK)] += back


def ffn_block_terms(col_index, row_count, full_tok, full_cot, gate_w, up_w, down_w):
    hblk, slots = col_index.shape
    rows, width = full_tok.shape
    wspec = pl.BlockSpec((1, slots, BLK, BLK), lambda h, c, n: (h, 0, 0, 0))
    full = pl.BlockSpec((rows, width), lambda h, c, n: (0, 0))
    grad = jax.ShapeDtypeStruct((hblk, slots, BLK, BLK), jnp.float32)
    flops = 2 * rows * hblk * slots * BLK * BLK * 9
    return pl.pallas_call(
        _ffn_kernel,
        grid_spec=pltpu.PrefetchScalarGridSpec(
            num_scalar_prefetch=2,
            grid=(hblk,),
            in_specs=[full, full, wspec, wspec, wspec],
            out_specs=[wspec, wspec, wspec, full],
        ),
        out_shape=[grad, grad, grad, jax.ShapeDtypeStruct((rows, width), jnp.float32)],
        compiler_params=pltpu.CompilerParams(dimension_semantics=("arbitrary",)),
        cost_estimate=pl.CostEstimate(
            flops=flops,
            transcendentals=rows * hblk * BLK,
            bytes_accessed=3 * hblk * slots * BLK * BLK * 6 + rows * width * 8,
        ),
        name="ffn_block_terms",
    )(col_index, row_count, full_tok, full_cot, gate_w, up_w, down_w)


def shards(n_dp, n_t, tokens, cotangent, w_gate, w_up, w_down, col_index, row_count, adam_m, adam_v):
    swap = [(0, 1), (1, 0)]
    first = lax.axis_index("tensor") == 0
    if n_t == 2:
        other_tok, other_cot = lax.ppermute((tokens, cotangent), "tensor", swap)
        full_tok = jnp.concatenate(
            [jnp.where(first, tokens, other_tok), jnp.where(first, other_tok, tokens)], axis=1
        )
        full_cot = jnp.concatenate(
            [jnp.where(first, cotangent, other_cot), jnp.where(first, other_cot, cotangent)], axis=1
        )
    else:
        full_tok = lax.all_gather(tokens, "tensor", axis=1, tiled=True)
        full_cot = lax.all_gather(cotangent, "tensor", axis=1, tiled=True)
    tok_rows = full_tok.shape[0]
    own_rows = w_gate.shape[1] * w_gate.shape[2] * BLK
    grad_gate, grad_up, grad_down, dx_part = ffn_block_terms(
        col_index, row_count, full_tok, full_cot, w_gate[0], w_up[0], w_down[0]
    )
    reduced = jnp.stack(
        ring_reduce_scatter(
            [g.reshape(own_rows, BLK) for g in (grad_gate, grad_up, grad_down)],
            n_dp,
            n_t,
            ring_order(n_dp),
            jnp.bfloat16,
        )
    )[:, None]
    if n_t == 2:
        half = tokens.shape[1]
        lo, hi = dx_part[:, :half], dx_part[:, half:]
        mine = jnp.where(first, lo, hi)
        theirs = lax.ppermute(jnp.where(first, hi, lo).astype(jnp.bfloat16), "tensor", swap)
        token_grads = (mine + theirs.astype(jnp.float32)).astype(jnp.bfloat16)
    else:
        token_grads = lax.psum_scatter(
            dx_part.astype(jnp.bfloat16), "tensor", scatter_dimension=1, tiled=True
        )
    grad_scale = 1.0 / math.sqrt(n_dp * tok_rows)
    grad_all = reduced * grad_scale
    m_new = 0.9 * adam_m + 0.1 * grad_all
    v_new = 0.95 * adam_v + 0.05 * grad_all * grad_all
    step_dir = m_new / (jnp.sqrt(v_new) + 1e-08)
    return (token_grads, m_new, v_new, step_dir)


def solution(mesh):
    in_specs = (
        P("dp", "tensor"),
        P("dp", "tensor"),
        P("tensor", None, None, None, None),
        P("tensor", None, None, None, None),
        P("tensor", None, None, None, None),
        P("tensor", None),
        P("tensor"),
        P(None, "tensor", "dp", None),
        P(None, "tensor", "dp", None),
    )
    out_specs = (
        P("dp", "tensor"),
        P(None, "tensor", "dp", None),
        P(None, "tensor", "dp", None),
        P(None, "tensor", "dp", None),
    )
    body = functools.partial(shards, mesh.shape["dp"], mesh.shape["tensor"])
    return jax.shard_map(body, mesh=mesh, in_specs=in_specs, out_specs=out_specs, check_vma=False)
```

```python
import functools
import math

import jax
import numpy as np
import jax.numpy as jnp
from jax import lax
from jax.experimental import pallas as pl
from jax.experimental.pallas import tpu as pltpu
from jax.sharding import PartitionSpec as P

D = 5120
BLK = 128


def ring_order(n):
    if n != 16:
        return list(range(n))
    plane = [(0, 0), (1, 0), (1, 1), (0, 1)]
    order = []
    for q, (x, y) in enumerate(plane):
        zs = range(4) if q % 2 == 0 else range(3, -1, -1)
        order += [z * 4 + y * 2 + x for z in zs]
    return order


def ring_reduce_scatter(streams, n, nt, order, wire_dtype):
    chunk = streams[0].shape[0] // n
    pos_of = [0] * n
    for p, d in enumerate(order):
        pos_of[d] = p
    table = np.zeros((n * nt, n), np.int32)
    for d in range(n):
        for t in range(nt):
            hop = 1 if t % 2 == 0 else -1
            for s in range(n):
                table[d * nt + t, s] = order[(pos_of[d] - hop * (1 + s)) % n] * chunk
    device = lax.axis_index("dp") * nt + lax.axis_index("tensor")
    offsets = jnp.asarray(table)[device]

    def own(full, s):
        return lax.dynamic_slice_in_dim(full, offsets[s], chunk, axis=0)

    perm = []
    for p in range(n):
        for t in range(nt):
            hop = 1 if t % 2 == 0 else -1
            perm.append((order[p] * nt + t, order[(p + hop) % n] * nt + t))
    accs = [own(full, 0) for full in streams]
    for s in range(1, n):
        for i, full in enumerate(streams):
            moved = lax.ppermute(accs[i].astype(wire_dtype), ("dp", "tensor"), perm)
            accs[i] = moved.astype(jnp.float32) + own(full, s)
    return accs


def _ffn_kernel(col_ref, cnt_ref, tok_ref, cot_ref, wg_ref, wu_ref, wd_ref,
                gg_ref, gu_ref, gd_ref, dx_ref):
    h = pl.program_id(0)
    slots = wg_ref.shape[1]
    count = cnt_ref[h]

    @pl.when(h == 0)
    def _():
        dx_ref[...] = jnp.zeros_like(dx_ref)

    offs, xs, dys, wgs, wus, wds = [], [], [], [], [], []
    for p in range(slots):
        off = pl.multiple_of(col_ref[h, p] * BLK, BLK)
        live = p < count
        offs.append(off)
        xs.append(tok_ref[:, pl.ds(off, BLK)])
        dys.append(cot_ref[:, pl.ds(off, BLK)])
        wgs.append(jnp.where(live, wg_ref[0, p], jnp.zeros_like(wg_ref[0, p])))
        wus.append(jnp.where(live, wu_ref[0, p], jnp.zeros_like(wu_ref[0, p])))
        wds.append(jnp.where(live, wd_ref[0, p], jnp.zeros_like(wd_ref[0, p])))
    f32 = jnp.float32
    nt = (((1,), (1,)), ((), ()))
    tn = (((0,), (0,)), ((), ()))
    gate = sum(jnp.dot(xs[p], wgs[p], preferred_element_type=f32) for p in range(slots))
    up = sum(jnp.dot(xs[p], wus[p], preferred_element_type=f32) for p in range(slots))
    d_hidden = sum(
        lax.dot_general(dys[p], wds[p], nt, preferred_element_type=f32) for p in range(slots)
    )
    sig = 1.0 / (1.0 + jnp.exp(-gate))
    silu = gate * sig
    hidden = (silu * up).astype(jnp.bfloat16)
    d_gate = (d_hidden * up * sig * (1.0 + gate * (1.0 - sig))).astype(jnp.bfloat16)
    d_up = (d_hidden * silu).astype(jnp.bfloat16)
    for p in range(slots):
        live = p < count
        zero = jnp.zeros((BLK, BLK), f32)
        gg = lax.dot_general(xs[p], d_gate, tn, preferred_element_type=f32)
        gu = lax.dot_general(xs[p], d_up, tn, preferred_element_type=f32)
        gd = lax.dot_general(hidden, dys[p], tn, preferred_element_type=f32)
        gg_ref[0, p] = jnp.where(live, gg, zero)
        gu_ref[0, p] = jnp.where(live, gu, zero)
        gd_ref[0, p] = jnp.where(live, gd, zero)
        back = lax.dot_general(d_gate, wgs[p], nt, preferred_element_type=f32)
        back = back + lax.dot_general(d_up, wus[p], nt, preferred_element_type=f32)
        dx_ref[:, pl.ds(offs[p], BLK)] += back


def ffn_block_terms(col_index, row_count, full_tok, full_cot, gate_w, up_w, down_w):
    hblk, slots = col_index.shape
    rows, width = full_tok.shape
    wspec = pl.BlockSpec((1, slots, BLK, BLK), lambda h, c, n: (h, 0, 0, 0))
    full = pl.BlockSpec((rows, width), lambda h, c, n: (0, 0))
    grad = jax.ShapeDtypeStruct((hblk, slots, BLK, BLK), jnp.float32)
    flops = 2 * rows * hblk * slots * BLK * BLK * 9
    return pl.pallas_call(
        _ffn_kernel,
        grid_spec=pltpu.PrefetchScalarGridSpec(
            num_scalar_prefetch=2,
            grid=(hblk,),
            in_specs=[full, full, wspec, wspec, wspec],
            out_specs=[wspec, wspec, wspec, full],
        ),
        out_shape=[grad, grad, grad, jax.ShapeDtypeStruct((rows, width), jnp.float32)],
        compiler_params=pltpu.CompilerParams(dimension_semantics=("arbitrary",)),
        cost_estimate=pl.CostEstimate(
            flops=flops,
            transcendentals=rows * hblk * BLK,
            bytes_accessed=3 * hblk * slots * BLK * BLK * 6 + rows * width * 8,
        ),
        name="ffn_block_terms",
    )(col_index, row_count, full_tok, full_cot, gate_w, up_w, down_w)


def shards(n_dp, n_t, tokens, cotangent, w_gate, w_up, w_down, col_index, row_count, adam_m, adam_v):
    swap = [(0, 1), (1, 0)]
    first = lax.axis_index("tensor") == 0
    if n_t == 2:
        other_tok, other_cot = lax.ppermute((tokens, cotangent), "tensor", swap)
        full_tok = jnp.concatenate(
            [jnp.where(first, tokens, other_tok), jnp.where(first, other_tok, tokens)], axis=1
        )
        full_cot = jnp.concatenate(
            [jnp.where(first, cotangent, other_cot), jnp.where(first, other_cot, cotangent)], axis=1
        )
    else:
        full_tok = lax.all_gather(tokens, "tensor", axis=1, tiled=True)
        full_cot = lax.all_gather(cotangent, "tensor", axis=1, tiled=True)
    tok_rows = full_tok.shape[0]
    own_rows = w_gate.shape[1] * w_gate.shape[2] * BLK
    grad_gate, grad_up, grad_down, dx_part = ffn_block_terms(
        col_index, row_count, full_tok, full_cot, w_gate[0], w_up[0], w_down[0]
    )
    reduced = jnp.stack(
        ring_reduce_scatter(
            [g.reshape(own_rows, BLK) for g in (grad_gate, grad_up, grad_down)],
            n_dp,
            n_t,
            ring_order(n_dp),
            jnp.bfloat16,
        )
    )[:, None]
    if n_t == 2:
        half = tokens.shape[1]
        lo, hi = dx_part[:, :half], dx_part[:, half:]
        mine = jnp.where(first, lo, hi)
        theirs = lax.ppermute(jnp.where(first, hi, lo).astype(jnp.bfloat16), "tensor", swap)
        token_grads = (mine + theirs.astype(jnp.float32)).astype(jnp.bfloat16)
    else:
        token_grads = lax.psum_scatter(
            dx_part.astype(jnp.bfloat16), "tensor", scatter_dimension=1, tiled=True
        )
    grad_scale = 1.0 / math.sqrt(n_dp * tok_rows)
    grad_all = reduced * grad_scale
    m_new = 0.9 * adam_m + 0.1 * grad_all
    v_new = 0.95 * adam_v + 0.05 * grad_all * grad_all
    step_dir = m_new / (jnp.sqrt(v_new) + 1e-08)
    return (token_grads, m_new, v_new, step_dir)


def solution(mesh):
    in_specs = (
        P("dp", "tensor"),
        P("dp", "tensor"),
        P("tensor", None, None, None, None),
        P("tensor", None, None, None, None),
        P("tensor", None, None, None, None),
        P("tensor", None),
        P("tensor"),
        P(None, "tensor", "dp", None),
        P(None, "tensor", "dp", None),
    )
    out_specs = (
        P("dp", "tensor"),
        P(None, "tensor", "dp", None),
        P(None, "tensor", "dp", None),
        P(None, "tensor", "dp", None),
    )
    body = functools.partial(shards, mesh.shape["dp"], mesh.shape["tensor"])
    return jax.shard_map(body, mesh=mesh, in_specs=in_specs, out_specs=out_specs, check_vma=False)
```

```python
import functools
import math

import jax
import jax.numpy as jnp
from jax import lax
from jax.experimental import pallas as pl
from jax.experimental.pallas import tpu as pltpu
from jax.sharding import PartitionSpec as P

D = 5120
BLK = 128


def ring_order(n):
    if n != 16:
        return list(range(n))
    plane = [(0, 0), (1, 0), (1, 1), (0, 1)]
    order = []
    for q, (x, y) in enumerate(plane):
        zs = range(4) if q % 2 == 0 else range(3, -1, -1)
        order += [z * 4 + y * 2 + x for z in zs]
    return order


def ring_reduce_scatter(streams, n, nt, order, wire_dtype):
    chunk = streams[0].shape[0] // n
    pos_of = [0] * n
    for p, d in enumerate(order):
        pos_of[d] = p
    me = jnp.asarray(pos_of, jnp.int32)[lax.axis_index("dp")]
    step = 1 - 2 * (lax.axis_index("tensor") % 2)
    order_arr = jnp.asarray(order, jnp.int32)

    def own(full, s):
        p = (me - step * (1 + s)) % n
        return lax.dynamic_slice_in_dim(full, order_arr[p] * chunk, chunk, axis=0)

    perm = []
    for p in range(n):
        for t in range(nt):
            hop = 1 if t % 2 == 0 else -1
            perm.append((order[p] * nt + t, order[(p + hop) % n] * nt + t))
    accs = [own(full, 0) for full in streams]
    for s in range(1, n):
        for i, full in enumerate(streams):
            moved = lax.ppermute(accs[i].astype(wire_dtype), ("dp", "tensor"), perm)
            accs[i] = moved.astype(jnp.float32) + own(full, s)
    return accs


def _ffn_kernel(col_ref, cnt_ref, tok_ref, cot_ref, tokt_ref, cott_ref, wg_ref, wu_ref, wdt_ref,
                gg_ref, gu_ref, gd_ref, dxt_ref):
    h = pl.program_id(0)
    slots = wg_ref.shape[1]
    count = cnt_ref[h]

    @pl.when(h == 0)
    def _():
        dxt_ref[...] = jnp.zeros_like(dxt_ref)

    f32 = jnp.float32
    offs, xs, dys, wgs, wus = [], [], [], [], []
    gate = up = d_hidden = None
    for p in range(slots):
        off = pl.multiple_of(col_ref[h, p] * BLK, BLK)
        live = p < count
        x = tok_ref[:, pl.ds(off, BLK)]
        dy = cot_ref[:, pl.ds(off, BLK)]
        wg = jnp.where(live, wg_ref[0, p], jnp.zeros_like(wg_ref[0, p]))
        wu = jnp.where(live, wu_ref[0, p], jnp.zeros_like(wu_ref[0, p]))
        wdt = jnp.where(live, wdt_ref[0, p], jnp.zeros_like(wdt_ref[0, p]))
        g = jnp.dot(x, wg, preferred_element_type=f32)
        u = jnp.dot(x, wu, preferred_element_type=f32)
        d = jnp.dot(dy, wdt, preferred_element_type=f32)
        gate = g if gate is None else gate + g
        up = u if up is None else up + u
        d_hidden = d if d_hidden is None else d_hidden + d
        offs.append(off)
        wgs.append(wg)
        wus.append(wu)
    sig = 1.0 / (1.0 + jnp.exp(-gate))
    silu = gate * sig
    hidden = (silu * up).astype(jnp.bfloat16)
    d_gate = (d_hidden * up * sig * (1.0 + gate * (1.0 - sig))).astype(jnp.bfloat16)
    d_up = (d_hidden * silu).astype(jnp.bfloat16)
    hidden_t = hidden.T
    d_gate_t = d_gate.T
    d_up_t = d_up.T
    for p in range(slots):
        live = p < count
        zero = jnp.zeros((BLK, BLK), f32)
        xt = tokt_ref[pl.ds(offs[p], BLK), :]
        dy = cot_ref[:, pl.ds(offs[p], BLK)]
        gg = jnp.dot(xt, d_gate, preferred_element_type=f32)
        gu = jnp.dot(xt, d_up, preferred_element_type=f32)
        gd = jnp.dot(hidden_t, dy, preferred_element_type=f32)
        gg_ref[0, p] = jnp.where(live, gg, zero)
        gu_ref[0, p] = jnp.where(live, gu, zero)
        gd_ref[0, p] = jnp.where(live, gd, zero)
        back_t = jnp.dot(wgs[p], d_gate_t, preferred_element_type=f32)
        back_t = back_t + jnp.dot(wus[p], d_up_t, preferred_element_type=f32)
        dxt_ref[pl.ds(offs[p], BLK), :] += back_t


def ffn_block_terms(col_index, row_count, full_tok, full_cot, gate_w, up_w, down_w):
    hblk, slots = col_index.shape
    rows, width = full_tok.shape
    down_t = jnp.swapaxes(down_w, 2, 3)
    wspec = pl.BlockSpec((1, slots, BLK, BLK), lambda h, c, n: (h, 0, 0, 0))
    full = pl.BlockSpec((rows, width), lambda h, c, n: (0, 0))
    full_t = pl.BlockSpec((width, rows), lambda h, c, n: (0, 0))
    grad = jax.ShapeDtypeStruct((hblk, slots, BLK, BLK), jnp.float32)
    flops = 2 * rows * hblk * slots * BLK * BLK * 9
    return pl.pallas_call(
        _ffn_kernel,
        grid_spec=pltpu.PrefetchScalarGridSpec(
            num_scalar_prefetch=2,
            grid=(hblk,),
            in_specs=[full, full, full_t, full_t, wspec, wspec, wspec],
            out_specs=[wspec, wspec, wspec, full_t],
        ),
        out_shape=[grad, grad, grad, jax.ShapeDtypeStruct((width, rows), jnp.float32)],
        compiler_params=pltpu.CompilerParams(dimension_semantics=("arbitrary",)),
        cost_estimate=pl.CostEstimate(
            flops=flops,
            transcendentals=rows * hblk * BLK,
            bytes_accessed=3 * hblk * slots * BLK * BLK * 6 + rows * width * 12,
        ),
        name="ffn_block_terms",
    )(col_index, row_count, full_tok, full_cot, full_tok.T, full_cot.T, gate_w, up_w, down_t)


def shards(n_dp, n_t, tokens, cotangent, w_gate, w_up, w_down, col_index, row_count, adam_m, adam_v):
    swap = [(0, 1), (1, 0)]
    first = lax.axis_index("tensor") == 0
    if n_t == 2:
        other_tok, other_cot = lax.ppermute((tokens, cotangent), "tensor", swap)
        full_tok = jnp.concatenate(
            [jnp.where(first, tokens, other_tok), jnp.where(first, other_tok, tokens)], axis=1
        )
        full_cot = jnp.concatenate(
            [jnp.where(first, cotangent, other_cot), jnp.where(first, other_cot, cotangent)], axis=1
        )
    else:
        full_tok = lax.all_gather(tokens, "tensor", axis=1, tiled=True)
        full_cot = lax.all_gather(cotangent, "tensor", axis=1, tiled=True)
    tok_rows = full_tok.shape[0]
    own_rows = w_gate.shape[1] * w_gate.shape[2] * BLK
    grad_gate, grad_up, grad_down, dx_part = ffn_block_terms(
        col_index, row_count, full_tok, full_cot, w_gate[0], w_up[0], w_down[0]
    )
    reduced = jnp.stack(
        ring_reduce_scatter(
            [g.reshape(own_rows, BLK) for g in (grad_gate, grad_up, grad_down)],
            n_dp,
            n_t,
            ring_order(n_dp),
            jnp.bfloat16,
        )
    )[:, None]
    if n_t == 2:
        half = tokens.shape[1]
        lo, hi = dx_part[:half].T, dx_part[half:].T
        mine = jnp.where(first, lo, hi)
        theirs = lax.ppermute(jnp.where(first, hi, lo).astype(jnp.bfloat16), "tensor", swap)
        token_grads = (mine + theirs.astype(jnp.float32)).astype(jnp.bfloat16)
    else:
        token_grads = lax.psum_scatter(
            dx_part.T.astype(jnp.bfloat16), "tensor", scatter_dimension=1, tiled=True
        )
    grad_scale = 1.0 / math.sqrt(n_dp * tok_rows)
    grad_all = reduced * grad_scale
    m_new = 0.9 * adam_m + 0.1 * grad_all
    v_new = 0.95 * adam_v + 0.05 * grad_all * grad_all
    step_dir = m_new / (jnp.sqrt(v_new) + 1e-08)
    return (token_grads, m_new, v_new, step_dir)


def solution(mesh):
    in_specs = (
        P("dp", "tensor"),
        P("dp", "tensor"),
        P("tensor", None, None, None, None),
        P("tensor", None, None, None, None),
        P("tensor", None, None, None, None),
        P("tensor", None),
        P("tensor"),
        P(None, "tensor", "dp", None),
        P(None, "tensor", "dp", None),
    )
    out_specs = (
        P("dp", "tensor"),
        P(None, "tensor", "dp", None),
        P(None, "tensor", "dp", None),
        P(None, "tensor", "dp", None),
    )
    body = functools.partial(shards, mesh.shape["dp"], mesh.shape["tensor"])
    return jax.shard_map(body, mesh=mesh, in_specs=in_specs, out_specs=out_specs, check_vma=False)
```

```python
import functools
import math

import jax
import jax.numpy as jnp
from jax import lax
from jax.experimental import pallas as pl
from jax.experimental.pallas import tpu as pltpu
from jax.sharding import PartitionSpec as P

D = 5120
BLK = 128


def ring_order(n):
    if n != 16:
        return list(range(n))
    plane = [(0, 0), (1, 0), (1, 1), (0, 1)]
    order = []
    for q, (x, y) in enumerate(plane):
        zs = range(4) if q % 2 == 0 else range(3, -1, -1)
        order += [z * 4 + y * 2 + x for z in zs]
    return order


def ring_reduce_scatter(streams, n, nt, order, wire_dtype):
    chunk = streams[0].shape[0] // n
    pos_of = [0] * n
    for p, d in enumerate(order):
        pos_of[d] = p
    me = jnp.asarray(pos_of, jnp.int32)[lax.axis_index("dp")]
    step = 1 - 2 * (lax.axis_index("tensor") % 2)
    order_arr = jnp.asarray(order, jnp.int32)

    def own(full, s):
        p = (me - step * (1 + s)) % n
        return lax.dynamic_slice_in_dim(full, order_arr[p] * chunk, chunk, axis=0)

    perm = []
    for p in range(n):
        for t in range(nt):
            hop = 1 if t % 2 == 0 else -1
            perm.append((order[p] * nt + t, order[(p + hop) % n] * nt + t))
    accs = [own(full, 0) for full in streams]
    for s in range(1, n):
        for i, full in enumerate(streams):
            moved = lax.ppermute(accs[i].astype(wire_dtype), ("dp", "tensor"), perm)
            accs[i] = moved.astype(jnp.float32) + own(full, s)
    return accs


def _ffn_kernel(col_ref, cnt_ref, tok_ref, cot_ref, wgu_ref, wdt_ref,
                gg_ref, gu_ref, gd_ref, dxt_ref):
    h = pl.program_id(0)
    slots = gg_ref.shape[1]
    count = cnt_ref[h]

    @pl.when(h == 0)
    def _():
        dxt_ref[...] = jnp.zeros_like(dxt_ref)

    f32 = jnp.float32
    offs = [pl.multiple_of(col_ref[h, p] * BLK, BLK) for p in range(slots)]
    x = jnp.concatenate([tok_ref[:, pl.ds(o, BLK)] for o in offs], axis=1)
    dy = jnp.concatenate([cot_ref[:, pl.ds(o, BLK)] for o in offs], axis=1)
    wgu = wgu_ref[0]
    wdt = wdt_ref[0]
    live_gu = lax.broadcasted_iota(jnp.int32, wgu.shape, 0) < count * BLK
    live_d = lax.broadcasted_iota(jnp.int32, wdt.shape, 0) < count * BLK
    wgu = jnp.where(live_gu, wgu, jnp.zeros_like(wgu))
    wdt = jnp.where(live_d, wdt, jnp.zeros_like(wdt))
    gate_up = jnp.dot(x, wgu, preferred_element_type=f32)
    gate, up = gate_up[:, :BLK], gate_up[:, BLK:]
    d_hidden = jnp.dot(dy, wdt, preferred_element_type=f32)
    sig = 1.0 / (1.0 + jnp.exp(-gate))
    silu = gate * sig
    hidden = (silu * up).astype(jnp.bfloat16)
    d_gate = (d_hidden * up * sig * (1.0 + gate * (1.0 - sig))).astype(jnp.bfloat16)
    d_up = (d_hidden * silu).astype(jnp.bfloat16)
    d_gu = jnp.concatenate([d_gate, d_up], axis=1)
    grad_gu = jnp.dot(x.T, d_gu, preferred_element_type=f32)
    grad_d = jnp.dot(hidden.T, dy, preferred_element_type=f32)
    back_t = jnp.dot(wgu, d_gu.T, preferred_element_type=f32)
    for p in range(slots):
        live = p < count
        zero = jnp.zeros((BLK, BLK), f32)
        rows = slice(p * BLK, (p + 1) * BLK)
        gg_ref[0, p] = jnp.where(live, grad_gu[rows, :BLK], zero)
        gu_ref[0, p] = jnp.where(live, grad_gu[rows, BLK:], zero)
        gd_ref[0, p] = jnp.where(live, grad_d[:, rows], zero)
        dxt_ref[pl.ds(offs[p], BLK), :] += back_t[rows]


def ffn_block_terms(col_index, row_count, full_tok, full_cot, gate_w, up_w, down_w):
    hblk, slots = col_index.shape
    rows, width = full_tok.shape
    wgu = jnp.concatenate([gate_w, up_w], axis=3).reshape(hblk, slots * BLK, 2 * BLK)
    wdt = jnp.swapaxes(down_w, 2, 3).reshape(hblk, slots * BLK, BLK)
    full = pl.BlockSpec((rows, width), lambda h, c, n: (0, 0))
    full_t = pl.BlockSpec((width, rows), lambda h, c, n: (0, 0))
    gspec = pl.BlockSpec((1, slots, BLK, BLK), lambda h, c, n: (h, 0, 0, 0))
    grad = jax.ShapeDtypeStruct((hblk, slots, BLK, BLK), jnp.float32)
    flops = 2 * rows * hblk * slots * BLK * BLK * 9
    return pl.pallas_call(
        _ffn_kernel,
        grid_spec=pltpu.PrefetchScalarGridSpec(
            num_scalar_prefetch=2,
            grid=(hblk,),
            in_specs=[
                full,
                full,
                pl.BlockSpec((1, slots * BLK, 2 * BLK), lambda h, c, n: (h, 0, 0)),
                pl.BlockSpec((1, slots * BLK, BLK), lambda h, c, n: (h, 0, 0)),
            ],
            out_specs=[gspec, gspec, gspec, full_t],
        ),
        out_shape=[grad, grad, grad, jax.ShapeDtypeStruct((width, rows), jnp.float32)],
        compiler_params=pltpu.CompilerParams(dimension_semantics=("arbitrary",)),
        cost_estimate=pl.CostEstimate(
            flops=flops,
            transcendentals=rows * hblk * BLK,
            bytes_accessed=3 * hblk * slots * BLK * BLK * 6 + rows * width * 8,
        ),
        name="ffn_block_terms",
    )(col_index, row_count, full_tok, full_cot, wgu, wdt)


def shards(n_dp, n_t, tokens, cotangent, w_gate, w_up, w_down, col_index, row_count, adam_m, adam_v):
    swap = [(0, 1), (1, 0)]
    first = lax.axis_index("tensor") == 0
    if n_t == 2:
        other_tok, other_cot = lax.ppermute((tokens, cotangent), "tensor", swap)
        full_tok = jnp.concatenate(
            [jnp.where(first, tokens, other_tok), jnp.where(first, other_tok, tokens)], axis=1
        )
        full_cot = jnp.concatenate(
            [jnp.where(first, cotangent, other_cot), jnp.where(first, other_cot, cotangent)], axis=1
        )
    else:
        full_tok = lax.all_gather(tokens, "tensor", axis=1, tiled=True)
        full_cot = lax.all_gather(cotangent, "tensor", axis=1, tiled=True)
    tok_rows = full_tok.shape[0]
    own_rows = w_gate.shape[1] * w_gate.shape[2] * BLK
    grad_gate, grad_up, grad_down, dx_part = ffn_block_terms(
        col_index, row_count, full_tok, full_cot, w_gate[0], w_up[0], w_down[0]
    )
    reduced = jnp.stack(
        ring_reduce_scatter(
            [g.reshape(own_rows, BLK) for g in (grad_gate, grad_up, grad_down)],
            n_dp,
            n_t,
            ring_order(n_dp),
            jnp.bfloat16,
        )
    )[:, None]
    if n_t == 2:
        half = tokens.shape[1]
        lo, hi = dx_part[:half].T, dx_part[half:].T
        mine = jnp.where(first, lo, hi)
        theirs = lax.ppermute(jnp.where(first, hi, lo).astype(jnp.bfloat16), "tensor", swap)
        token_grads = (mine + theirs.astype(jnp.float32)).astype(jnp.bfloat16)
    else:
        token_grads = lax.psum_scatter(
            dx_part.T.astype(jnp.bfloat16), "tensor", scatter_dimension=1, tiled=True
        )
    grad_scale = 1.0 / math.sqrt(n_dp * tok_rows)
    grad_all = reduced * grad_scale
    m_new = 0.9 * adam_m + 0.1 * grad_all
    v_new = 0.95 * adam_v + 0.05 * grad_all * grad_all
    step_dir = m_new / (jnp.sqrt(v_new) + 1e-08)
    return (token_grads, m_new, v_new, step_dir)


def solution(mesh):
    in_specs = (
        P("dp", "tensor"),
        P("dp", "tensor"),
        P("tensor", None, None, None, None),
        P("tensor", None, None, None, None),
        P("tensor", None, None, None, None),
        P("tensor", None),
        P("tensor"),
        P(None, "tensor", "dp", None),
        P(None, "tensor", "dp", None),
    )
    out_specs = (
        P("dp", "tensor"),
        P(None, "tensor", "dp", None),
        P(None, "tensor", "dp", None),
        P(None, "tensor", "dp", None),
    )
    body = functools.partial(shards, mesh.shape["dp"], mesh.shape["tensor"])
    return jax.shard_map(body, mesh=mesh, in_specs=in_specs, out_specs=out_specs, check_vma=False)
```

```python
import functools
import math

import jax
import jax.numpy as jnp
from jax import lax
from jax.experimental import pallas as pl
from jax.experimental.pallas import tpu as pltpu
from jax.sharding import PartitionSpec as P

D = 5120
BLK = 128


def ring_order(n):
    if n != 16:
        return list(range(n))
    plane = [(0, 0), (1, 0), (1, 1), (0, 1)]
    order = []
    for q, (x, y) in enumerate(plane):
        zs = range(4) if q % 2 == 0 else range(3, -1, -1)
        order += [z * 4 + y * 2 + x for z in zs]
    return order


def ring_reduce_scatter(streams, n, nt, order, wire_dtype):
    chunk = streams[0].shape[0] // n
    pos_of = [0] * n
    for p, d in enumerate(order):
        pos_of[d] = p
    me = jnp.asarray(pos_of, jnp.int32)[lax.axis_index("dp")]
    step = 1 - 2 * (lax.axis_index("tensor") % 2)
    order_arr = jnp.asarray(order, jnp.int32)

    def own(full, s):
        p = (me - step * (1 + s)) % n
        return lax.dynamic_slice_in_dim(full, order_arr[p] * chunk, chunk, axis=0)

    perm = []
    for p in range(n):
        for t in range(nt):
            hop = 1 if t % 2 == 0 else -1
            perm.append((order[p] * nt + t, order[(p + hop) % n] * nt + t))
    accs = [own(full, 0) for full in streams]
    for s in range(1, n):
        for i, full in enumerate(streams):
            moved = lax.ppermute(accs[i].astype(wire_dtype), ("dp", "tensor"), perm)
            accs[i] = moved.astype(jnp.float32) + own(full, s)
    return accs


def _ffn_kernel(col_ref, cnt_ref, tok_ref, cot_ref, wg_ref, wu_ref, wd_ref,
                gg_ref, gu_ref, gd_ref, dxt_ref):
    h = pl.program_id(0)
    slots = gg_ref.shape[1]
    count = cnt_ref[h]

    @pl.when(h == 0)
    def _():
        dxt_ref[...] = jnp.zeros_like(dxt_ref)

    f32 = jnp.float32
    offs = [pl.multiple_of(col_ref[h, p] * BLK, BLK) for p in range(slots)]
    x = jnp.concatenate([tok_ref[:, pl.ds(o, BLK)] for o in offs], axis=1)
    dy = jnp.concatenate([cot_ref[:, pl.ds(o, BLK)] for o in offs], axis=1)
    stacked = (slots * BLK, BLK)
    live_rows = lax.broadcasted_iota(jnp.int32, stacked, 0) < count * BLK
    wg = wg_ref[0].reshape(stacked)
    wu = wu_ref[0].reshape(stacked)
    wg = jnp.where(live_rows, wg, jnp.zeros_like(wg))
    wu = jnp.where(live_rows, wu, jnp.zeros_like(wu))
    wd = jnp.concatenate([wd_ref[0, p] for p in range(slots)], axis=1)
    live_cols = lax.broadcasted_iota(jnp.int32, wd.shape, 1) < count * BLK
    wd = jnp.where(live_cols, wd, jnp.zeros_like(wd))
    gate = jnp.dot(x, wg, preferred_element_type=f32)
    up = jnp.dot(x, wu, preferred_element_type=f32)
    d_hidden = lax.dot_general(dy, wd, (((1,), (1,)), ((), ())), preferred_element_type=f32)
    sig = 1.0 / (1.0 + jnp.exp(-gate))
    silu = gate * sig
    hidden = (silu * up).astype(jnp.bfloat16)
    d_gate = (d_hidden * up * sig * (1.0 + gate * (1.0 - sig))).astype(jnp.bfloat16)
    d_up = (d_hidden * silu).astype(jnp.bfloat16)
    d_gu = jnp.concatenate([d_gate, d_up], axis=1)
    grad_gu = jnp.dot(x.T, d_gu, preferred_element_type=f32)
    grad_d = jnp.dot(hidden.T, dy, preferred_element_type=f32)
    back_t = jnp.dot(wg, d_gate.T, preferred_element_type=f32)
    back_t = back_t + jnp.dot(wu, d_up.T, preferred_element_type=f32)
    for p in range(slots):
        live = p < count
        zero = jnp.zeros((BLK, BLK), f32)
        rows = slice(p * BLK, (p + 1) * BLK)
        gg_ref[0, p] = jnp.where(live, grad_gu[rows, :BLK], zero)
        gu_ref[0, p] = jnp.where(live, grad_gu[rows, BLK:], zero)
        gd_ref[0, p] = jnp.where(live, grad_d[:, rows], zero)
        dxt_ref[pl.ds(offs[p], BLK), :] += back_t[rows]


def ffn_block_terms(col_index, row_count, full_tok, full_cot, gate_w, up_w, down_w):
    hblk, slots = col_index.shape
    rows, width = full_tok.shape
    wspec = pl.BlockSpec((1, slots, BLK, BLK), lambda h, c, n: (h, 0, 0, 0))
    full = pl.BlockSpec((rows, width), lambda h, c, n: (0, 0))
    full_t = pl.BlockSpec((width, rows), lambda h, c, n: (0, 0))
    gspec = pl.BlockSpec((1, slots, BLK, BLK), lambda h, c, n: (h, 0, 0, 0))
    grad = jax.ShapeDtypeStruct((hblk, slots, BLK, BLK), jnp.float32)
    flops = 2 * rows * hblk * slots * BLK * BLK * 9
    return pl.pallas_call(
        _ffn_kernel,
        grid_spec=pltpu.PrefetchScalarGridSpec(
            num_scalar_prefetch=2,
            grid=(hblk,),
            in_specs=[full, full, wspec, wspec, wspec],
            out_specs=[gspec, gspec, gspec, full_t],
        ),
        out_shape=[grad, grad, grad, jax.ShapeDtypeStruct((width, rows), jnp.float32)],
        compiler_params=pltpu.CompilerParams(dimension_semantics=("arbitrary",)),
        cost_estimate=pl.CostEstimate(
            flops=flops,
            transcendentals=rows * hblk * BLK,
            bytes_accessed=3 * hblk * slots * BLK * BLK * 6 + rows * width * 8,
        ),
        name="ffn_block_terms",
    )(col_index, row_count, full_tok, full_cot, gate_w, up_w, down_w)


def shards(n_dp, n_t, tokens, cotangent, w_gate, w_up, w_down, col_index, row_count, adam_m, adam_v):
    swap = [(0, 1), (1, 0)]
    first = lax.axis_index("tensor") == 0
    if n_t == 2:
        other_tok, other_cot = lax.ppermute((tokens, cotangent), "tensor", swap)
        full_tok = jnp.concatenate(
            [jnp.where(first, tokens, other_tok), jnp.where(first, other_tok, tokens)], axis=1
        )
        full_cot = jnp.concatenate(
            [jnp.where(first, cotangent, other_cot), jnp.where(first, other_cot, cotangent)], axis=1
        )
    else:
        full_tok = lax.all_gather(tokens, "tensor", axis=1, tiled=True)
        full_cot = lax.all_gather(cotangent, "tensor", axis=1, tiled=True)
    tok_rows = full_tok.shape[0]
    own_rows = w_gate.shape[1] * w_gate.shape[2] * BLK
    grad_gate, grad_up, grad_down, dx_part = ffn_block_terms(
        col_index, row_count, full_tok, full_cot, w_gate[0], w_up[0], w_down[0]
    )
    reduced = jnp.stack(
        ring_reduce_scatter(
            [g.reshape(own_rows, BLK) for g in (grad_gate, grad_up, grad_down)],
            n_dp,
            n_t,
            ring_order(n_dp),
            jnp.bfloat16,
        )
    )[:, None]
    if n_t == 2:
        half = tokens.shape[1]
        lo, hi = dx_part[:half].T, dx_part[half:].T
        mine = jnp.where(first, lo, hi)
        theirs = lax.ppermute(jnp.where(first, hi, lo).astype(jnp.bfloat16), "tensor", swap)
        token_grads = (mine + theirs.astype(jnp.float32)).astype(jnp.bfloat16)
    else:
        token_grads = lax.psum_scatter(
            dx_part.T.astype(jnp.bfloat16), "tensor", scatter_dimension=1, tiled=True
        )
    grad_scale = 1.0 / math.sqrt(n_dp * tok_rows)
    grad_all = reduced * grad_scale
    m_new = 0.9 * adam_m + 0.1 * grad_all
    v_new = 0.95 * adam_v + 0.05 * grad_all * grad_all
    step_dir = m_new / (jnp.sqrt(v_new) + 1e-08)
    return (token_grads, m_new, v_new, step_dir)


def solution(mesh):
    in_specs = (
        P("dp", "tensor"),
        P("dp", "tensor"),
        P("tensor", None, None, None, None),
        P("tensor", None, None, None, None),
        P("tensor", None, None, None, None),
        P("tensor", None),
        P("tensor"),
        P(None, "tensor", "dp", None),
        P(None, "tensor", "dp", None),
    )
    out_specs = (
        P("dp", "tensor"),
        P(None, "tensor", "dp", None),
        P(None, "tensor", "dp", None),
        P(None, "tensor", "dp", None),
    )
    body = functools.partial(shards, mesh.shape["dp"], mesh.shape["tensor"])
    return jax.shard_map(body, mesh=mesh, in_specs=in_specs, out_specs=out_specs, check_vma=False)
```

```python
import functools
import math

import jax
import jax.numpy as jnp
from jax import lax
from jax.experimental import pallas as pl
from jax.experimental.pallas import tpu as pltpu
from jax.sharding import PartitionSpec as P

D = 5120
BLK = 128


def ring_order(n):
    if n != 16:
        return list(range(n))
    plane = [(0, 0), (1, 0), (1, 1), (0, 1)]
    order = []
    for q, (x, y) in enumerate(plane):
        zs = range(4) if q % 2 == 0 else range(3, -1, -1)
        order += [z * 4 + y * 2 + x for z in zs]
    return order


def ring_reduce_scatter(streams, n, nt, order, wire_dtype):
    chunk = streams[0].shape[0] // n
    pos_of = [0] * n
    for p, d in enumerate(order):
        pos_of[d] = p
    me = jnp.asarray(pos_of, jnp.int32)[lax.axis_index("dp")]
    step = 1 - 2 * (lax.axis_index("tensor") % 2)
    order_arr = jnp.asarray(order, jnp.int32)

    def own(full, s):
        p = (me - step * (1 + s)) % n
        return lax.dynamic_slice_in_dim(full, order_arr[p] * chunk, chunk, axis=0)

    perm = []
    for p in range(n):
        for t in range(nt):
            hop = 1 if t % 2 == 0 else -1
            perm.append((order[p] * nt + t, order[(p + hop) % n] * nt + t))
    accs = [own(full, 0) for full in streams]
    for s in range(1, n):
        for i, full in enumerate(streams):
            moved = lax.ppermute(accs[i].astype(wire_dtype), ("dp", "tensor"), perm)
            accs[i] = moved.astype(jnp.float32) + own(full, s)
    return accs


def _ffn_block(hh, h, count, col_ref, tok_ref, cot_ref, wg_ref, wu_ref, wd_ref,
               gg_ref, gu_ref, gd_ref, dxt_ref):
    slots = gg_ref.shape[1]
    f32 = jnp.float32
    offs = [pl.multiple_of(col_ref[h, p] * BLK, BLK) for p in range(slots)]
    x = jnp.concatenate([tok_ref[:, pl.ds(o, BLK)] for o in offs], axis=1)
    dy = jnp.concatenate([cot_ref[:, pl.ds(o, BLK)] for o in offs], axis=1)
    stacked = (slots * BLK, BLK)
    live_rows = lax.broadcasted_iota(jnp.int32, stacked, 0) < count * BLK
    wg = wg_ref[hh].reshape(stacked)
    wu = wu_ref[hh].reshape(stacked)
    wg = jnp.where(live_rows, wg, jnp.zeros_like(wg))
    wu = jnp.where(live_rows, wu, jnp.zeros_like(wu))
    wd = jnp.concatenate([wd_ref[hh, p] for p in range(slots)], axis=1)
    live_cols = lax.broadcasted_iota(jnp.int32, wd.shape, 1) < count * BLK
    wd = jnp.where(live_cols, wd, jnp.zeros_like(wd))
    gate = jnp.dot(x, wg, preferred_element_type=f32)
    up = jnp.dot(x, wu, preferred_element_type=f32)
    d_hidden = lax.dot_general(dy, wd, (((1,), (1,)), ((), ())), preferred_element_type=f32)
    sig = 1.0 / (1.0 + jnp.exp(-gate))
    silu = gate * sig
    hidden = (silu * up).astype(jnp.bfloat16)
    d_gate = (d_hidden * up * sig * (1.0 + gate * (1.0 - sig))).astype(jnp.bfloat16)
    d_up = (d_hidden * silu).astype(jnp.bfloat16)
    d_gu = jnp.concatenate([d_gate, d_up], axis=1)
    grad_gu = jnp.dot(x.T, d_gu, preferred_element_type=f32)
    grad_d = jnp.dot(hidden.T, dy, preferred_element_type=f32)
    back_t = jnp.dot(wg, d_gate.T, preferred_element_type=f32)
    back_t = back_t + jnp.dot(wu, d_up.T, preferred_element_type=f32)
    for p in range(slots):
        live = p < count
        zero = jnp.zeros((BLK, BLK), f32)
        rows = slice(p * BLK, (p + 1) * BLK)
        gg_ref[hh, p] = jnp.where(live, grad_gu[rows, :BLK], zero)
        gu_ref[hh, p] = jnp.where(live, grad_gu[rows, BLK:], zero)
        gd_ref[hh, p] = jnp.where(live, grad_d[:, rows], zero)
        dxt_ref[pl.ds(offs[p], BLK), :] += back_t[rows]


def _ffn_kernel(col_ref, cnt_ref, tok_ref, cot_ref, wg_ref, wu_ref, wd_ref,
                gg_ref, gu_ref, gd_ref, dxt_ref):
    step = pl.program_id(0)
    per_step = gg_ref.shape[0]

    @pl.when(step == 0)
    def _():
        dxt_ref[...] = jnp.zeros_like(dxt_ref)

    for hh in range(per_step):
        h = step * per_step + hh
        _ffn_block(hh, h, cnt_ref[h], col_ref, tok_ref, cot_ref, wg_ref, wu_ref, wd_ref,
                   gg_ref, gu_ref, gd_ref, dxt_ref)


def ffn_block_terms(col_index, row_count, full_tok, full_cot, gate_w, up_w, down_w):
    hblk, slots = col_index.shape
    rows, width = full_tok.shape
    per_step = 3 if hblk % 3 == 0 else 1
    wspec = pl.BlockSpec((per_step, slots, BLK, BLK), lambda h, c, n: (h, 0, 0, 0))
    full = pl.BlockSpec((rows, width), lambda h, c, n: (0, 0))
    full_t = pl.BlockSpec((width, rows), lambda h, c, n: (0, 0))
    gspec = wspec
    grad = jax.ShapeDtypeStruct((hblk, slots, BLK, BLK), jnp.float32)
    flops = 2 * rows * hblk * slots * BLK * BLK * 9
    return pl.pallas_call(
        _ffn_kernel,
        grid_spec=pltpu.PrefetchScalarGridSpec(
            num_scalar_prefetch=2,
            grid=(hblk // per_step,),
            in_specs=[full, full, wspec, wspec, wspec],
            out_specs=[gspec, gspec, gspec, full_t],
        ),
        out_shape=[grad, grad, grad, jax.ShapeDtypeStruct((width, rows), jnp.float32)],
        compiler_params=pltpu.CompilerParams(dimension_semantics=("arbitrary",)),
        cost_estimate=pl.CostEstimate(
            flops=flops,
            transcendentals=rows * hblk * BLK,
            bytes_accessed=3 * hblk * slots * BLK * BLK * 6 + rows * width * 8,
        ),
        name="ffn_block_terms",
    )(col_index, row_count, full_tok, full_cot, gate_w, up_w, down_w)


def shards(n_dp, n_t, tokens, cotangent, w_gate, w_up, w_down, col_index, row_count, adam_m, adam_v):
    swap = [(0, 1), (1, 0)]
    first = lax.axis_index("tensor") == 0
    if n_t == 2:
        other_tok, other_cot = lax.ppermute((tokens, cotangent), "tensor", swap)
        full_tok = jnp.concatenate(
            [jnp.where(first, tokens, other_tok), jnp.where(first, other_tok, tokens)], axis=1
        )
        full_cot = jnp.concatenate(
            [jnp.where(first, cotangent, other_cot), jnp.where(first, other_cot, cotangent)], axis=1
        )
    else:
        full_tok = lax.all_gather(tokens, "tensor", axis=1, tiled=True)
        full_cot = lax.all_gather(cotangent, "tensor", axis=1, tiled=True)
    tok_rows = full_tok.shape[0]
    own_rows = w_gate.shape[1] * w_gate.shape[2] * BLK
    grad_gate, grad_up, grad_down, dx_part = ffn_block_terms(
        col_index, row_count, full_tok, full_cot, w_gate[0], w_up[0], w_down[0]
    )
    reduced = jnp.stack(
        ring_reduce_scatter(
            [g.reshape(own_rows, BLK) for g in (grad_gate, grad_up, grad_down)],
            n_dp,
            n_t,
            ring_order(n_dp),
            jnp.bfloat16,
        )
    )[:, None]
    if n_t == 2:
        half = tokens.shape[1]
        lo, hi = dx_part[:half].T, dx_part[half:].T
        mine = jnp.where(first, lo, hi)
        theirs = lax.ppermute(jnp.where(first, hi, lo).astype(jnp.bfloat16), "tensor", swap)
        token_grads = (mine + theirs.astype(jnp.float32)).astype(jnp.bfloat16)
    else:
        token_grads = lax.psum_scatter(
            dx_part.T.astype(jnp.bfloat16), "tensor", scatter_dimension=1, tiled=True
        )
    grad_scale = 1.0 / math.sqrt(n_dp * tok_rows)
    grad_all = reduced * grad_scale
    m_new = 0.9 * adam_m + 0.1 * grad_all
    v_new = 0.95 * adam_v + 0.05 * grad_all * grad_all
    step_dir = m_new / (jnp.sqrt(v_new) + 1e-08)
    return (token_grads, m_new, v_new, step_dir)


def solution(mesh):
    in_specs = (
        P("dp", "tensor"),
        P("dp", "tensor"),
        P("tensor", None, None, None, None),
        P("tensor", None, None, None, None),
        P("tensor", None, None, None, None),
        P("tensor", None),
        P("tensor"),
        P(None, "tensor", "dp", None),
        P(None, "tensor", "dp", None),
    )
    out_specs = (
        P("dp", "tensor"),
        P(None, "tensor", "dp", None),
        P(None, "tensor", "dp", None),
        P(None, "tensor", "dp", None),
    )
    body = functools.partial(shards, mesh.shape["dp"], mesh.shape["tensor"])
    return jax.shard_map(body, mesh=mesh, in_specs=in_specs, out_specs=out_specs, check_vma=False)
```

```python
import functools
import math

import jax
import jax.numpy as jnp
from jax import lax
from jax.experimental import pallas as pl
from jax.experimental.pallas import tpu as pltpu
from jax.sharding import PartitionSpec as P

D = 5120
BLK = 128


def ring_order(n):
    if n != 16:
        return list(range(n))
    plane = [(0, 0), (1, 0), (1, 1), (0, 1)]
    order = []
    for q, (x, y) in enumerate(plane):
        zs = range(4) if q % 2 == 0 else range(3, -1, -1)
        order += [z * 4 + y * 2 + x for z in zs]
    return order


def ring_reduce_scatter(streams, n, nt, order, wire_dtype):
    chunk = streams[0].shape[0] // n
    pos_of = [0] * n
    for p, d in enumerate(order):
        pos_of[d] = p
    me = jnp.asarray(pos_of, jnp.int32)[lax.axis_index("dp")]
    step = 1 - 2 * (lax.axis_index("tensor") % 2)
    order_arr = jnp.asarray(order, jnp.int32)

    def own(full, s):
        p = (me - step * (1 + s)) % n
        return lax.dynamic_slice_in_dim(full, order_arr[p] * chunk, chunk, axis=0)

    perm = []
    for p in range(n):
        for t in range(nt):
            hop = 1 if t % 2 == 0 else -1
            perm.append((order[p] * nt + t, order[(p + hop) % n] * nt + t))
    accs = [own(full, 0) for full in streams]
    for s in range(1, n):
        for i, full in enumerate(streams):
            moved = lax.ppermute(accs[i].astype(wire_dtype), ("dp", "tensor"), perm)
            accs[i] = moved.astype(jnp.float32) + own(full, s)
    return accs


def _ffn_block(hh, h, count, col_ref, tok_ref, cot_ref, wg_ref, wu_ref, wd_ref,
               gg_ref, gu_ref, gd_ref, dxt_ref):
    slots = gg_ref.shape[1]
    f32 = jnp.float32
    offs = [pl.multiple_of(col_ref[h, p] * BLK, BLK) for p in range(slots)]
    x = jnp.concatenate([tok_ref[:, pl.ds(o, BLK)] for o in offs], axis=1)
    dy = jnp.concatenate([cot_ref[:, pl.ds(o, BLK)] for o in offs], axis=1)
    stacked = (slots * BLK, BLK)
    live_rows = lax.broadcasted_iota(jnp.int32, stacked, 0) < count * BLK
    wg = wg_ref[hh].reshape(stacked)
    wu = wu_ref[hh].reshape(stacked)
    wg = jnp.where(live_rows, wg, jnp.zeros_like(wg))
    wu = jnp.where(live_rows, wu, jnp.zeros_like(wu))
    wd = jnp.concatenate([wd_ref[hh, p] for p in range(slots)], axis=1)
    live_cols = lax.broadcasted_iota(jnp.int32, wd.shape, 1) < count * BLK
    wd = jnp.where(live_cols, wd, jnp.zeros_like(wd))
    gate = jnp.dot(x, wg, preferred_element_type=f32)
    up = jnp.dot(x, wu, preferred_element_type=f32)
    d_hidden = lax.dot_general(dy, wd, (((1,), (1,)), ((), ())), preferred_element_type=f32)
    sig = 1.0 / (1.0 + jnp.exp(-gate))
    silu = gate * sig
    hidden = (silu * up).astype(jnp.bfloat16)
    d_gate = (d_hidden * up * sig * (1.0 + gate * (1.0 - sig))).astype(jnp.bfloat16)
    d_up = (d_hidden * silu).astype(jnp.bfloat16)
    d_gu = jnp.concatenate([d_gate, d_up], axis=1)
    grad_gu = jnp.dot(x.T, d_gu, preferred_element_type=f32)
    grad_d = jnp.dot(hidden.T, dy, preferred_element_type=f32)
    back_t = jnp.dot(wg, d_gate.T, preferred_element_type=f32)
    back_t = back_t + jnp.dot(wu, d_up.T, preferred_element_type=f32)
    for p in range(slots):
        live = p < count
        zero = jnp.zeros((BLK, BLK), f32)
        rows = slice(p * BLK, (p + 1) * BLK)
        gg_ref[hh, p] = jnp.where(live, grad_gu[rows, :BLK], zero)
        gu_ref[hh, p] = jnp.where(live, grad_gu[rows, BLK:], zero)
        gd_ref[hh, p] = jnp.where(live, grad_d[:, rows], zero)
        dxt_ref[pl.ds(offs[p], BLK), :] += back_t[rows]


def _ffn_kernel(col_ref, cnt_ref, tok_ref, cot_ref, wg_ref, wu_ref, wd_ref,
                gg_ref, gu_ref, gd_ref, dxt_ref):
    step = pl.program_id(0)
    per_step = gg_ref.shape[0]

    @pl.when(step == 0)
    def _():
        dxt_ref[...] = jnp.zeros_like(dxt_ref)

    for hh in range(per_step):
        h = step * per_step + hh
        _ffn_block(hh, h, cnt_ref[h], col_ref, tok_ref, cot_ref, wg_ref, wu_ref, wd_ref,
                   gg_ref, gu_ref, gd_ref, dxt_ref)


def ffn_block_terms(col_index, row_count, full_tok, full_cot, gate_w, up_w, down_w):
    hblk, slots = col_index.shape
    rows, width = full_tok.shape
    per_step = 9 if hblk % 9 == 0 else (3 if hblk % 3 == 0 else 1)
    wspec = pl.BlockSpec((per_step, slots, BLK, BLK), lambda h, c, n: (h, 0, 0, 0))
    full = pl.BlockSpec((rows, width), lambda h, c, n: (0, 0))
    full_t = pl.BlockSpec((width, rows), lambda h, c, n: (0, 0))
    gspec = wspec
    grad = jax.ShapeDtypeStruct((hblk, slots, BLK, BLK), jnp.float32)
    flops = 2 * rows * hblk * slots * BLK * BLK * 9
    return pl.pallas_call(
        _ffn_kernel,
        grid_spec=pltpu.PrefetchScalarGridSpec(
            num_scalar_prefetch=2,
            grid=(hblk // per_step,),
            in_specs=[full, full, wspec, wspec, wspec],
            out_specs=[gspec, gspec, gspec, full_t],
        ),
        out_shape=[grad, grad, grad, jax.ShapeDtypeStruct((width, rows), jnp.float32)],
        compiler_params=pltpu.CompilerParams(dimension_semantics=("arbitrary",)),
        cost_estimate=pl.CostEstimate(
            flops=flops,
            transcendentals=rows * hblk * BLK,
            bytes_accessed=3 * hblk * slots * BLK * BLK * 6 + rows * width * 8,
        ),
        name="ffn_block_terms",
    )(col_index, row_count, full_tok, full_cot, gate_w, up_w, down_w)


def shards(n_dp, n_t, tokens, cotangent, w_gate, w_up, w_down, col_index, row_count, adam_m, adam_v):
    swap = [(0, 1), (1, 0)]
    first = lax.axis_index("tensor") == 0
    if n_t == 2:
        other_tok, other_cot = lax.ppermute((tokens, cotangent), "tensor", swap)
        full_tok = jnp.concatenate(
            [jnp.where(first, tokens, other_tok), jnp.where(first, other_tok, tokens)], axis=1
        )
        full_cot = jnp.concatenate(
            [jnp.where(first, cotangent, other_cot), jnp.where(first, other_cot, cotangent)], axis=1
        )
    else:
        full_tok = lax.all_gather(tokens, "tensor", axis=1, tiled=True)
        full_cot = lax.all_gather(cotangent, "tensor", axis=1, tiled=True)
    tok_rows = full_tok.shape[0]
    own_rows = w_gate.shape[1] * w_gate.shape[2] * BLK
    grad_gate, grad_up, grad_down, dx_part = ffn_block_terms(
        col_index, row_count, full_tok, full_cot, w_gate[0], w_up[0], w_down[0]
    )
    reduced = jnp.stack(
        ring_reduce_scatter(
            [g.reshape(own_rows, BLK) for g in (grad_gate, grad_up, grad_down)],
            n_dp,
            n_t,
            ring_order(n_dp),
            jnp.bfloat16,
        )
    )[:, None]
    if n_t == 2:
        half = tokens.shape[1]
        lo, hi = dx_part[:half].T, dx_part[half:].T
        mine = jnp.where(first, lo, hi)
        theirs = lax.ppermute(jnp.where(first, hi, lo).astype(jnp.bfloat16), "tensor", swap)
        token_grads = (mine + theirs.astype(jnp.float32)).astype(jnp.bfloat16)
    else:
        token_grads = lax.psum_scatter(
            dx_part.T.astype(jnp.bfloat16), "tensor", scatter_dimension=1, tiled=True
        )
    grad_scale = 1.0 / math.sqrt(n_dp * tok_rows)
    grad_all = reduced * grad_scale
    m_new = 0.9 * adam_m + 0.1 * grad_all
    v_new = 0.95 * adam_v + 0.05 * grad_all * grad_all
    step_dir = m_new / (jnp.sqrt(v_new) + 1e-08)
    return (token_grads, m_new, v_new, step_dir)


def solution(mesh):
    in_specs = (
        P("dp", "tensor"),
        P("dp", "tensor"),
        P("tensor", None, None, None, None),
        P("tensor", None, None, None, None),
        P("tensor", None, None, None, None),
        P("tensor", None),
        P("tensor"),
        P(None, "tensor", "dp", None),
        P(None, "tensor", "dp", None),
    )
    out_specs = (
        P("dp", "tensor"),
        P(None, "tensor", "dp", None),
        P(None, "tensor", "dp", None),
        P(None, "tensor", "dp", None),
    )
    body = functools.partial(shards, mesh.shape["dp"], mesh.shape["tensor"])
    return jax.shard_map(body, mesh=mesh, in_specs=in_specs, out_specs=out_specs, check_vma=False)
```

```python
import functools
import math

import jax
import jax.numpy as jnp
from jax import lax
from jax.experimental import pallas as pl
from jax.experimental.pallas import tpu as pltpu
from jax.sharding import PartitionSpec as P

D = 5120
BLK = 128


def ring_order(n):
    if n != 16:
        return list(range(n))
    plane = [(0, 0), (1, 0), (1, 1), (0, 1)]
    order = []
    for q, (x, y) in enumerate(plane):
        zs = range(4) if q % 2 == 0 else range(3, -1, -1)
        order += [z * 4 + y * 2 + x for z in zs]
    return order


def ring_reduce_scatter(streams, n, nt, order, wire_dtype):
    chunk = streams[0].shape[0] // n
    pos_of = [0] * n
    for p, d in enumerate(order):
        pos_of[d] = p
    me = jnp.asarray(pos_of, jnp.int32)[lax.axis_index("dp")]
    step = 1 - 2 * (lax.axis_index("tensor") % 2)
    order_arr = jnp.asarray(order, jnp.int32)

    def own(full, s):
        p = (me - step * (1 + s)) % n
        return lax.dynamic_slice_in_dim(full, order_arr[p] * chunk, chunk, axis=0)

    perm = []
    for p in range(n):
        for t in range(nt):
            hop = 1 if t % 2 == 0 else -1
            perm.append((order[p] * nt + t, order[(p + hop) % n] * nt + t))
    accs = [own(full, 0) for full in streams]
    for s in range(1, n):
        for i, full in enumerate(streams):
            moved = lax.ppermute(accs[i].astype(wire_dtype), ("dp", "tensor"), perm)
            accs[i] = moved.astype(jnp.float32) + own(full, s)
    return accs


def _slot_offsets(col_ref, h, slots):
    return [pl.multiple_of(col_ref[h, p] * BLK, BLK) for p in range(slots)]


def _stacked(w_ref, hh, count, slots):
    w = w_ref[hh].reshape(slots * BLK, BLK)
    live = lax.broadcasted_iota(jnp.int32, w.shape, 0) < count * BLK
    return jnp.where(live, w, jnp.zeros_like(w))


def _forward_kernel(col_ref, cnt_ref, tok_ref, cot_ref, wg_ref, wu_ref, wd_ref, gd_ref, dgu_ref):
    step = pl.program_id(0)
    per_step, slots = gd_ref.shape[0], gd_ref.shape[1]
    f32 = jnp.float32
    for hh in range(per_step):
        h = step * per_step + hh
        count = cnt_ref[h]
        offs = _slot_offsets(col_ref, h, slots)
        x = jnp.concatenate([tok_ref[:, pl.ds(o, BLK)] for o in offs], axis=1)
        dy = jnp.concatenate([cot_ref[:, pl.ds(o, BLK)] for o in offs], axis=1)
        wg = _stacked(wg_ref, hh, count, slots)
        wu = _stacked(wu_ref, hh, count, slots)
        wd = jnp.concatenate([wd_ref[hh, p] for p in range(slots)], axis=1)
        live_cols = lax.broadcasted_iota(jnp.int32, wd.shape, 1) < count * BLK
        wd = jnp.where(live_cols, wd, jnp.zeros_like(wd))
        gate = jnp.dot(x, wg, preferred_element_type=f32)
        up = jnp.dot(x, wu, preferred_element_type=f32)
        d_hidden = lax.dot_general(dy, wd, (((1,), (1,)), ((), ())), preferred_element_type=f32)
        sig = 1.0 / (1.0 + jnp.exp(-gate))
        silu = gate * sig
        hidden = (silu * up).astype(jnp.bfloat16)
        d_gate = (d_hidden * up * sig * (1.0 + gate * (1.0 - sig))).astype(jnp.bfloat16)
        d_up = (d_hidden * silu).astype(jnp.bfloat16)
        dgu_ref[hh] = jnp.concatenate([d_gate, d_up], axis=1)
        grad_d = jnp.dot(hidden.T, dy, preferred_element_type=f32)
        zero = jnp.zeros((BLK, BLK), f32)
        for p in range(slots):
            gd_ref[hh, p] = jnp.where(p < count, grad_d[:, p * BLK:(p + 1) * BLK], zero)


def _backward_kernel(col_ref, cnt_ref, tok_ref, dgu_ref, wg_ref, wu_ref, gg_ref, gu_ref, dxt_ref):
    step = pl.program_id(0)
    per_step, slots = gg_ref.shape[0], gg_ref.shape[1]
    f32 = jnp.float32

    @pl.when(step == 0)
    def _():
        dxt_ref[...] = jnp.zeros_like(dxt_ref)

    for hh in range(per_step):
        h = step * per_step + hh
        count = cnt_ref[h]
        offs = _slot_offsets(col_ref, h, slots)
        x = jnp.concatenate([tok_ref[:, pl.ds(o, BLK)] for o in offs], axis=1)
        wg = _stacked(wg_ref, hh, count, slots)
        wu = _stacked(wu_ref, hh, count, slots)
        d_gu = dgu_ref[hh]
        grad_gu = jnp.dot(x.T, d_gu, preferred_element_type=f32)
        back_t = jnp.dot(wg, d_gu[:, :BLK].T, preferred_element_type=f32)
        back_t = back_t + jnp.dot(wu, d_gu[:, BLK:].T, preferred_element_type=f32)
        zero = jnp.zeros((BLK, BLK), f32)
        for p in range(slots):
            rows = slice(p * BLK, (p + 1) * BLK)
            gg_ref[hh, p] = jnp.where(p < count, grad_gu[rows, :BLK], zero)
            gu_ref[hh, p] = jnp.where(p < count, grad_gu[rows, BLK:], zero)
            dxt_ref[pl.ds(offs[p], BLK), :] += back_t[rows]


def ffn_block_terms(col_index, row_count, full_tok, full_cot, gate_w, up_w, down_w):
    hblk, slots = col_index.shape
    rows, width = full_tok.shape
    per_step = 9 if hblk % 9 == 0 else (3 if hblk % 3 == 0 else 1)
    wspec = pl.BlockSpec((per_step, slots, BLK, BLK), lambda h, c, n: (h, 0, 0, 0))
    dspec = pl.BlockSpec((per_step, rows, 2 * BLK), lambda h, c, n: (h, 0, 0))
    full = pl.BlockSpec((rows, width), lambda h, c, n: (0, 0))
    full_t = pl.BlockSpec((width, rows), lambda h, c, n: (0, 0))
    grad = jax.ShapeDtypeStruct((hblk, slots, BLK, BLK), jnp.float32)
    dgu = jax.ShapeDtypeStruct((hblk, rows, 2 * BLK), jnp.bfloat16)
    unit = 2 * rows * hblk * slots * BLK * BLK
    params = pltpu.CompilerParams(dimension_semantics=("arbitrary",))
    grad_down, d_gu = pl.pallas_call(
        _forward_kernel,
        grid_spec=pltpu.PrefetchScalarGridSpec(
            num_scalar_prefetch=2,
            grid=(hblk // per_step,),
            in_specs=[full, full, wspec, wspec, wspec],
            out_specs=[wspec, dspec],
        ),
        out_shape=[grad, dgu],
        compiler_params=params,
        cost_estimate=pl.CostEstimate(
            flops=4 * unit,
            transcendentals=rows * hblk * BLK,
            bytes_accessed=hblk * slots * BLK * BLK * 10 + rows * width * 4,
        ),
        name="ffn_forward_terms",
    )(col_index, row_count, full_tok, full_cot, gate_w, up_w, down_w)
    grad_gate, grad_up, dx_t = pl.pallas_call(
        _backward_kernel,
        grid_spec=pltpu.PrefetchScalarGridSpec(
            num_scalar_prefetch=2,
            grid=(hblk // per_step,),
            in_specs=[full, dspec, wspec, wspec],
            out_specs=[wspec, wspec, full_t],
        ),
        out_shape=[grad, grad, jax.ShapeDtypeStruct((width, rows), jnp.float32)],
        compiler_params=params,
        cost_estimate=pl.CostEstimate(
            flops=5 * unit,
            transcendentals=0,
            bytes_accessed=hblk * slots * BLK * BLK * 12 + rows * width * 6,
        ),
        name="ffn_backward_terms",
    )(col_index, row_count, full_tok, d_gu, gate_w, up_w)
    return grad_gate, grad_up, grad_down, dx_t


def shards(n_dp, n_t, tokens, cotangent, w_gate, w_up, w_down, col_index, row_count, adam_m, adam_v):
    swap = [(0, 1), (1, 0)]
    first = lax.axis_index("tensor") == 0
    if n_t == 2:
        other_tok, other_cot = lax.ppermute((tokens, cotangent), "tensor", swap)
        full_tok = jnp.concatenate(
            [jnp.where(first, tokens, other_tok), jnp.where(first, other_tok, tokens)], axis=1
        )
        full_cot = jnp.concatenate(
            [jnp.where(first, cotangent, other_cot), jnp.where(first, other_cot, cotangent)], axis=1
        )
    else:
        full_tok = lax.all_gather(tokens, "tensor", axis=1, tiled=True)
        full_cot = lax.all_gather(cotangent, "tensor", axis=1, tiled=True)
    tok_rows = full_tok.shape[0]
    own_rows = w_gate.shape[1] * w_gate.shape[2] * BLK
    grad_gate, grad_up, grad_down, dx_part = ffn_block_terms(
        col_index, row_count, full_tok, full_cot, w_gate[0], w_up[0], w_down[0]
    )
    red_down, red_gate, red_up = ring_reduce_scatter(
        [g.reshape(own_rows, BLK) for g in (grad_down, grad_gate, grad_up)],
        n_dp,
        n_t,
        ring_order(n_dp),
        jnp.bfloat16,
    )
    reduced = jnp.stack([red_gate, red_up, red_down])[:, None]
    if n_t == 2:
        half = tokens.shape[1]
        lo, hi = dx_part[:half].T, dx_part[half:].T
        mine = jnp.where(first, lo, hi)
        theirs = lax.ppermute(jnp.where(first, hi, lo).astype(jnp.bfloat16), "tensor", swap)
        token_grads = (mine + theirs.astype(jnp.float32)).astype(jnp.bfloat16)
    else:
        token_grads = lax.psum_scatter(
            dx_part.T.astype(jnp.bfloat16), "tensor", scatter_dimension=1, tiled=True
        )
    grad_scale = 1.0 / math.sqrt(n_dp * tok_rows)
    grad_all = reduced * grad_scale
    m_new = 0.9 * adam_m + 0.1 * grad_all
    v_new = 0.95 * adam_v + 0.05 * grad_all * grad_all
    step_dir = m_new / (jnp.sqrt(v_new) + 1e-08)
    return (token_grads, m_new, v_new, step_dir)


def solution(mesh):
    in_specs = (
        P("dp", "tensor"),
        P("dp", "tensor"),
        P("tensor", None, None, None, None),
        P("tensor", None, None, None, None),
        P("tensor", None, None, None, None),
        P("tensor", None),
        P("tensor"),
        P(None, "tensor", "dp", None),
        P(None, "tensor", "dp", None),
    )
    out_specs = (
        P("dp", "tensor"),
        P(None, "tensor", "dp", None),
        P(None, "tensor", "dp", None),
        P(None, "tensor", "dp", None),
    )
    body = functools.partial(shards, mesh.shape["dp"], mesh.shape["tensor"])
    return jax.shard_map(body, mesh=mesh, in_specs=in_specs, out_specs=out_specs, check_vma=False)
```

```python
import functools
import math

import jax
import jax.numpy as jnp
from jax import lax
from jax.experimental import pallas as pl
from jax.experimental.pallas import tpu as pltpu
from jax.sharding import PartitionSpec as P

D = 5120
BLK = 128


def ring_order(n):
    if n != 16:
        return list(range(n))
    plane = [(0, 0), (1, 0), (1, 1), (0, 1)]
    order = []
    for q, (x, y) in enumerate(plane):
        zs = range(4) if q % 2 == 0 else range(3, -1, -1)
        order += [z * 4 + y * 2 + x for z in zs]
    return order


def ring_reduce_scatter(streams, n, nt, order, wire_dtype):
    chunk = streams[0].shape[0] // n
    pos_of = [0] * n
    for p, d in enumerate(order):
        pos_of[d] = p
    me = jnp.asarray(pos_of, jnp.int32)[lax.axis_index("dp")]
    step = 1 - 2 * (lax.axis_index("tensor") % 2)
    order_arr = jnp.asarray(order, jnp.int32)

    def own(full, s):
        p = (me - step * (1 + s)) % n
        return lax.dynamic_slice_in_dim(full, order_arr[p] * chunk, chunk, axis=0)

    perm = []
    for p in range(n):
        for t in range(nt):
            hop = 1 if t % 2 == 0 else -1
            perm.append((order[p] * nt + t, order[(p + hop) % n] * nt + t))
    accs = [own(full, 0) for full in streams]
    for s in range(1, n):
        for i, full in enumerate(streams):
            moved = lax.ppermute(accs[i].astype(wire_dtype), ("dp", "tensor"), perm)
            accs[i] = moved.astype(jnp.float32) + own(full, s)
    return accs


def _ffn_block(hh, h, count, col_ref, tok_ref, cot_ref, wg_ref, wu_ref, wd_ref,
               gg_ref, gu_ref, gd_ref, dxt_ref):
    slots = gg_ref.shape[1]
    f32 = jnp.float32
    offs = [pl.multiple_of(col_ref[h, p] * BLK, BLK) for p in range(slots)]
    x = jnp.concatenate([tok_ref[:, pl.ds(o, BLK)] for o in offs], axis=1)
    dy = jnp.concatenate([cot_ref[:, pl.ds(o, BLK)] for o in offs], axis=1)
    stacked = (slots * BLK, BLK)
    live_rows = lax.broadcasted_iota(jnp.int32, stacked, 0) < count * BLK
    wg = wg_ref[hh].reshape(stacked)
    wu = wu_ref[hh].reshape(stacked)
    wg = jnp.where(live_rows, wg, jnp.zeros_like(wg))
    wu = jnp.where(live_rows, wu, jnp.zeros_like(wu))
    wd = jnp.concatenate([wd_ref[hh, p] for p in range(slots)], axis=1)
    live_cols = lax.broadcasted_iota(jnp.int32, wd.shape, 1) < count * BLK
    wd = jnp.where(live_cols, wd, jnp.zeros_like(wd))
    gate = jnp.dot(x, wg, preferred_element_type=f32)
    up = jnp.dot(x, wu, preferred_element_type=f32)
    d_hidden = lax.dot_general(dy, wd, (((1,), (1,)), ((), ())), preferred_element_type=f32)
    sig = 1.0 / (1.0 + jnp.exp(-gate))
    silu = gate * sig
    hidden = (silu * up).astype(jnp.bfloat16)
    d_gate = (d_hidden * up * sig * (1.0 + gate * (1.0 - sig))).astype(jnp.bfloat16)
    d_up = (d_hidden * silu).astype(jnp.bfloat16)
    d_gu = jnp.concatenate([d_gate, d_up], axis=1)
    grad_gu = jnp.dot(x.T, d_gu, preferred_element_type=f32)
    grad_d = jnp.dot(hidden.T, dy, preferred_element_type=f32)
    back_t = jnp.dot(wg, d_gate.T, preferred_element_type=f32)
    back_t = back_t + jnp.dot(wu, d_up.T, preferred_element_type=f32)
    for p in range(slots):
        live = p < count
        zero = jnp.zeros((BLK, BLK), f32)
        rows = slice(p * BLK, (p + 1) * BLK)
        gg_ref[hh, p] = jnp.where(live, grad_gu[rows, :BLK], zero)
        gu_ref[hh, p] = jnp.where(live, grad_gu[rows, BLK:], zero)
        gd_ref[hh, p] = jnp.where(live, grad_d[:, rows], zero)
        dxt_ref[pl.ds(offs[p], BLK), :] += back_t[rows]


def _ffn_kernel(col_ref, cnt_ref, tok_ref, cot_ref, wg_ref, wu_ref, wd_ref,
                gg_ref, gu_ref, gd_ref, dxt_ref):
    step = pl.program_id(0)
    per_step = gg_ref.shape[0]

    @pl.when(step == 0)
    def _():
        dxt_ref[...] = jnp.zeros_like(dxt_ref)

    for hh in range(per_step):
        h = step * per_step + hh
        _ffn_block(hh, h, cnt_ref[h], col_ref, tok_ref, cot_ref, wg_ref, wu_ref, wd_ref,
                   gg_ref, gu_ref, gd_ref, dxt_ref)


def ffn_block_terms(col_index, row_count, full_tok, full_cot, gate_w, up_w, down_w):
    hblk, slots = col_index.shape
    rows, width = full_tok.shape
    per_step = 9 if hblk % 9 == 0 else (3 if hblk % 3 == 0 else 1)
    wspec = pl.BlockSpec((per_step, slots, BLK, BLK), lambda h, c, n: (h, 0, 0, 0))
    full = pl.BlockSpec((rows, width), lambda h, c, n: (0, 0))
    full_t = pl.BlockSpec((width, rows), lambda h, c, n: (0, 0))
    gspec = wspec
    grad = jax.ShapeDtypeStruct((hblk, slots, BLK, BLK), jnp.float32)
    flops = 2 * rows * hblk * slots * BLK * BLK * 9
    return pl.pallas_call(
        _ffn_kernel,
        grid_spec=pltpu.PrefetchScalarGridSpec(
            num_scalar_prefetch=2,
            grid=(hblk // per_step,),
            in_specs=[full, full, wspec, wspec, wspec],
            out_specs=[gspec, gspec, gspec, full_t],
        ),
        out_shape=[grad, grad, grad, jax.ShapeDtypeStruct((width, rows), jnp.float32)],
        compiler_params=pltpu.CompilerParams(dimension_semantics=("arbitrary",)),
        cost_estimate=pl.CostEstimate(
            flops=flops,
            transcendentals=rows * hblk * BLK,
            bytes_accessed=3 * hblk * slots * BLK * BLK * 6 + rows * width * 8,
        ),
        name="ffn_block_terms",
    )(col_index, row_count, full_tok, full_cot, gate_w, up_w, down_w)


def shards(n_dp, n_t, tokens, cotangent, w_gate, w_up, w_down, col_index, row_count, adam_m, adam_v):
    swap = [(0, 1), (1, 0)]
    first = lax.axis_index("tensor") == 0
    if n_t == 2:
        other_tok, other_cot = lax.ppermute(jnp.stack([tokens, cotangent]), "tensor", swap)
        full_tok = jnp.concatenate(
            [jnp.where(first, tokens, other_tok), jnp.where(first, other_tok, tokens)], axis=1
        )
        full_cot = jnp.concatenate(
            [jnp.where(first, cotangent, other_cot), jnp.where(first, other_cot, cotangent)], axis=1
        )
    else:
        full_tok = lax.all_gather(tokens, "tensor", axis=1, tiled=True)
        full_cot = lax.all_gather(cotangent, "tensor", axis=1, tiled=True)
    tok_rows = full_tok.shape[0]
    own_rows = w_gate.shape[1] * w_gate.shape[2] * BLK
    grad_gate, grad_up, grad_down, dx_part = ffn_block_terms(
        col_index, row_count, full_tok, full_cot, w_gate[0], w_up[0], w_down[0]
    )
    reduced = jnp.stack(
        ring_reduce_scatter(
            [g.reshape(own_rows, BLK) for g in (grad_gate, grad_up, grad_down)],
            n_dp,
            n_t,
            ring_order(n_dp),
            jnp.bfloat16,
        )
    )[:, None]
    if n_t == 2:
        half = tokens.shape[1]
        lo, hi = dx_part[:half].T, dx_part[half:].T
        mine = jnp.where(first, lo, hi)
        theirs = lax.ppermute(jnp.where(first, hi, lo).astype(jnp.bfloat16), "tensor", swap)
        token_grads = (mine + theirs.astype(jnp.float32)).astype(jnp.bfloat16)
    else:
        token_grads = lax.psum_scatter(
            dx_part.T.astype(jnp.bfloat16), "tensor", scatter_dimension=1, tiled=True
        )
    grad_scale = 1.0 / math.sqrt(n_dp * tok_rows)
    grad_all = reduced * grad_scale
    m_new = 0.9 * adam_m + 0.1 * grad_all
    v_new = 0.95 * adam_v + 0.05 * grad_all * grad_all
    step_dir = m_new / (jnp.sqrt(v_new) + 1e-08)
    return (token_grads, m_new, v_new, step_dir)


def solution(mesh):
    in_specs = (
        P("dp", "tensor"),
        P("dp", "tensor"),
        P("tensor", None, None, None, None),
        P("tensor", None, None, None, None),
        P("tensor", None, None, None, None),
        P("tensor", None),
        P("tensor"),
        P(None, "tensor", "dp", None),
        P(None, "tensor", "dp", None),
    )
    out_specs = (
        P("dp", "tensor"),
        P(None, "tensor", "dp", None),
        P(None, "tensor", "dp", None),
        P(None, "tensor", "dp", None),
    )
    body = functools.partial(shards, mesh.shape["dp"], mesh.shape["tensor"])
    return jax.shard_map(body, mesh=mesh, in_specs=in_specs, out_specs=out_specs, check_vma=False)
```

```python
import functools
import math

import jax
import jax.numpy as jnp
from jax import lax
from jax.experimental import pallas as pl
from jax.experimental.pallas import tpu as pltpu
from jax.sharding import PartitionSpec as P

D = 5120
BLK = 128


def ring_order(n):
    if n != 16:
        return list(range(n))
    plane = [(0, 0), (1, 0), (1, 1), (0, 1)]
    order = []
    for q, (x, y) in enumerate(plane):
        zs = range(4) if q % 2 == 0 else range(3, -1, -1)
        order += [z * 4 + y * 2 + x for z in zs]
    return order


def ring_reduce_scatter(streams, n, nt, order, wire_dtype):
    chunk = streams[0].shape[0] // n
    pos_of = [0] * n
    for p, d in enumerate(order):
        pos_of[d] = p
    me = jnp.asarray(pos_of, jnp.int32)[lax.axis_index("dp")]
    step = 1 - 2 * (lax.axis_index("tensor") % 2)
    order_arr = jnp.asarray(order, jnp.int32)

    def own(full, s):
        p = (me - step * (1 + s)) % n
        return lax.dynamic_slice_in_dim(full, order_arr[p] * chunk, chunk, axis=0)

    perm = []
    for p in range(n):
        for t in range(nt):
            hop = 1 if t % 2 == 0 else -1
            perm.append((order[p] * nt + t, order[(p + hop) % n] * nt + t))
    accs = [own(full, 0) for full in streams]
    for s in range(1, n):
        for i, full in enumerate(streams):
            moved = lax.ppermute(accs[i].astype(wire_dtype), ("dp", "tensor"), perm)
            accs[i] = moved.astype(jnp.float32) + own(full, s)
    return accs


def _pick(own_ref, other_ref, use_other, off):
    return jnp.where(use_other, other_ref[:, pl.ds(off, BLK)], own_ref[:, pl.ds(off, BLK)])


def _ffn_block(hh, h, count, col_ref, loc_ref, src_ref, tok_ref, cot_ref, otok_ref, ocot_ref,
               wg_ref, wu_ref, wd_ref, gg_ref, gu_ref, gd_ref, dxt_ref):
    slots = gg_ref.shape[1]
    f32 = jnp.float32
    offs = [pl.multiple_of(col_ref[h, p] * BLK, BLK) for p in range(slots)]
    locs = [pl.multiple_of(loc_ref[h, p] * BLK, BLK) for p in range(slots)]
    far = [src_ref[h, p] != 0 for p in range(slots)]
    x = jnp.concatenate([_pick(tok_ref, otok_ref, f, o) for f, o in zip(far, locs)], axis=1)
    dy = jnp.concatenate([_pick(cot_ref, ocot_ref, f, o) for f, o in zip(far, locs)], axis=1)
    stacked = (slots * BLK, BLK)
    live_rows = lax.broadcasted_iota(jnp.int32, stacked, 0) < count * BLK
    wg = wg_ref[hh].reshape(stacked)
    wu = wu_ref[hh].reshape(stacked)
    wg = jnp.where(live_rows, wg, jnp.zeros_like(wg))
    wu = jnp.where(live_rows, wu, jnp.zeros_like(wu))
    wd = jnp.concatenate([wd_ref[hh, p] for p in range(slots)], axis=1)
    live_cols = lax.broadcasted_iota(jnp.int32, wd.shape, 1) < count * BLK
    wd = jnp.where(live_cols, wd, jnp.zeros_like(wd))
    gate = jnp.dot(x, wg, preferred_element_type=f32)
    up = jnp.dot(x, wu, preferred_element_type=f32)
    d_hidden = lax.dot_general(dy, wd, (((1,), (1,)), ((), ())), preferred_element_type=f32)
    sig = 1.0 / (1.0 + jnp.exp(-gate))
    silu = gate * sig
    hidden = (silu * up).astype(jnp.bfloat16)
    d_gate = (d_hidden * up * sig * (1.0 + gate * (1.0 - sig))).astype(jnp.bfloat16)
    d_up = (d_hidden * silu).astype(jnp.bfloat16)
    d_gu = jnp.concatenate([d_gate, d_up], axis=1)
    grad_gu = jnp.dot(x.T, d_gu, preferred_element_type=f32)
    grad_d = jnp.dot(hidden.T, dy, preferred_element_type=f32)
    back_t = jnp.dot(wg, d_gate.T, preferred_element_type=f32)
    back_t = back_t + jnp.dot(wu, d_up.T, preferred_element_type=f32)
    for p in range(slots):
        live = p < count
        zero = jnp.zeros((BLK, BLK), f32)
        rows = slice(p * BLK, (p + 1) * BLK)
        gg_ref[hh, p] = jnp.where(live, grad_gu[rows, :BLK], zero)
        gu_ref[hh, p] = jnp.where(live, grad_gu[rows, BLK:], zero)
        gd_ref[hh, p] = jnp.where(live, grad_d[:, rows], zero)
        dxt_ref[pl.ds(offs[p], BLK), :] += back_t[rows]


def _ffn_kernel(col_ref, loc_ref, src_ref, cnt_ref, tok_ref, cot_ref, otok_ref, ocot_ref,
                wg_ref, wu_ref, wd_ref, gg_ref, gu_ref, gd_ref, dxt_ref):
    step = pl.program_id(0)
    per_step = gg_ref.shape[0]

    @pl.when(step == 0)
    def _():
        dxt_ref[...] = jnp.zeros_like(dxt_ref)

    for hh in range(per_step):
        h = step * per_step + hh
        _ffn_block(hh, h, cnt_ref[h], col_ref, loc_ref, src_ref, tok_ref, cot_ref, otok_ref,
                   ocot_ref, wg_ref, wu_ref, wd_ref, gg_ref, gu_ref, gd_ref, dxt_ref)


def ffn_block_terms(col_index, col_local, col_far, row_count, tok, cot, other_tok, other_cot,
                    gate_w, up_w, down_w):
    hblk, slots = col_index.shape
    rows, part = tok.shape
    width = part * (2 if other_tok is not tok else 1)
    per_step = 9 if hblk % 9 == 0 else (3 if hblk % 3 == 0 else 1)
    wspec = pl.BlockSpec((per_step, slots, BLK, BLK), lambda h, c, l, s, n: (h, 0, 0, 0))
    full = pl.BlockSpec((rows, part), lambda h, c, l, s, n: (0, 0))
    full_t = pl.BlockSpec((width, rows), lambda h, c, l, s, n: (0, 0))
    gspec = wspec
    grad = jax.ShapeDtypeStruct((hblk, slots, BLK, BLK), jnp.float32)
    flops = 2 * rows * hblk * slots * BLK * BLK * 9
    return pl.pallas_call(
        _ffn_kernel,
        grid_spec=pltpu.PrefetchScalarGridSpec(
            num_scalar_prefetch=4,
            grid=(hblk // per_step,),
            in_specs=[full, full, full, full, wspec, wspec, wspec],
            out_specs=[gspec, gspec, gspec, full_t],
        ),
        out_shape=[grad, grad, grad, jax.ShapeDtypeStruct((width, rows), jnp.float32)],
        compiler_params=pltpu.CompilerParams(dimension_semantics=("arbitrary",)),
        cost_estimate=pl.CostEstimate(
            flops=flops,
            transcendentals=rows * hblk * BLK,
            bytes_accessed=3 * hblk * slots * BLK * BLK * 6 + rows * width * 8,
        ),
        name="ffn_block_terms",
    )(col_index, col_local, col_far, row_count, tok, cot, other_tok, other_cot, gate_w, up_w, down_w)


def shards(n_dp, n_t, tokens, cotangent, w_gate, w_up, w_down, col_index, row_count, adam_m, adam_v):
    swap = [(0, 1), (1, 0)]
    first = lax.axis_index("tensor") == 0
    if n_t == 2:
        other_tok, other_cot = lax.ppermute(jnp.stack([tokens, cotangent]), "tensor", swap)
        half_blocks = tokens.shape[1] // BLK
        col_local = col_index % half_blocks
        col_far = (col_index // half_blocks != lax.axis_index("tensor")).astype(jnp.int32)
        halves = (tokens, cotangent, other_tok, other_cot)
    else:
        full_tok = lax.all_gather(tokens, "tensor", axis=1, tiled=True)
        full_cot = lax.all_gather(cotangent, "tensor", axis=1, tiled=True)
        col_local, col_far = col_index, jnp.zeros_like(col_index)
        halves = (full_tok, full_cot, full_tok, full_cot)
    tok_rows = tokens.shape[0]
    own_rows = w_gate.shape[1] * w_gate.shape[2] * BLK
    grad_gate, grad_up, grad_down, dx_part = ffn_block_terms(
        col_index, col_local, col_far, row_count, *halves, w_gate[0], w_up[0], w_down[0]
    )
    reduced = jnp.stack(
        ring_reduce_scatter(
            [g.reshape(own_rows, BLK) for g in (grad_gate, grad_up, grad_down)],
            n_dp,
            n_t,
            ring_order(n_dp),
            jnp.bfloat16,
        )
    )[:, None]
    if n_t == 2:
        half = tokens.shape[1]
        lo, hi = dx_part[:half].T, dx_part[half:].T
        mine = jnp.where(first, lo, hi)
        theirs = lax.ppermute(jnp.where(first, hi, lo).astype(jnp.bfloat16), "tensor", swap)
        token_grads = (mine + theirs.astype(jnp.float32)).astype(jnp.bfloat16)
    else:
        token_grads = lax.psum_scatter(
            dx_part.T.astype(jnp.bfloat16), "tensor", scatter_dimension=1, tiled=True
        )
    grad_scale = 1.0 / math.sqrt(n_dp * tok_rows)
    grad_all = reduced * grad_scale
    m_new = 0.9 * adam_m + 0.1 * grad_all
    v_new = 0.95 * adam_v + 0.05 * grad_all * grad_all
    step_dir = m_new / (jnp.sqrt(v_new) + 1e-08)
    return (token_grads, m_new, v_new, step_dir)


def solution(mesh):
    in_specs = (
        P("dp", "tensor"),
        P("dp", "tensor"),
        P("tensor", None, None, None, None),
        P("tensor", None, None, None, None),
        P("tensor", None, None, None, None),
        P("tensor", None),
        P("tensor"),
        P(None, "tensor", "dp", None),
        P(None, "tensor", "dp", None),
    )
    out_specs = (
        P("dp", "tensor"),
        P(None, "tensor", "dp", None),
        P(None, "tensor", "dp", None),
        P(None, "tensor", "dp", None),
    )
    body = functools.partial(shards, mesh.shape["dp"], mesh.shape["tensor"])
    return jax.shard_map(body, mesh=mesh, in_specs=in_specs, out_specs=out_specs, check_vma=False)
```

```python
import functools
import math

import jax
import jax.numpy as jnp
from jax import lax
from jax.experimental import pallas as pl
from jax.experimental.pallas import tpu as pltpu
from jax.sharding import PartitionSpec as P

D = 5120
BLK = 128


def ring_order(n):
    if n != 16:
        return list(range(n))
    plane = [(0, 0), (1, 0), (1, 1), (0, 1)]
    order = []
    for q, (x, y) in enumerate(plane):
        zs = range(4) if q % 2 == 0 else range(3, -1, -1)
        order += [z * 4 + y * 2 + x for z in zs]
    return order


def ring_reduce_scatter(streams, n, nt, order, wire_dtype):
    chunk = streams[0].shape[0] // n
    pos_of = [0] * n
    for p, d in enumerate(order):
        pos_of[d] = p
    me = jnp.asarray(pos_of, jnp.int32)[lax.axis_index("dp")]
    step = 1 - 2 * (lax.axis_index("tensor") % 2)
    order_arr = jnp.asarray(order, jnp.int32)

    def own(full, s):
        p = (me - step * (1 + s)) % n
        return lax.dynamic_slice_in_dim(full, order_arr[p] * chunk, chunk, axis=0)

    perm = []
    for p in range(n):
        for t in range(nt):
            hop = 1 if t % 2 == 0 else -1
            perm.append((order[p] * nt + t, order[(p + hop) % n] * nt + t))
    accs = [own(full, 0) for full in streams]
    for s in range(1, n):
        for i, full in enumerate(streams):
            moved = lax.ppermute(accs[i].astype(wire_dtype), ("dp", "tensor"), perm)
            accs[i] = moved.astype(jnp.float32) + own(full, s)
    return accs


def _ffn_block(hh, h, count, col_ref, tok_ref, cot_ref, wg_ref, wu_ref, wd_ref,
               gg_ref, gu_ref, gd_ref, dxt_ref):
    slots = gg_ref.shape[1]
    f32 = jnp.float32
    offs = [pl.multiple_of(col_ref[p, h] * BLK, BLK) for p in range(slots)]
    x = jnp.concatenate([tok_ref[:, pl.ds(o, BLK)] for o in offs], axis=1)
    dy = jnp.concatenate([cot_ref[:, pl.ds(o, BLK)] for o in offs], axis=1)
    stacked = (slots * BLK, BLK)
    live_rows = lax.broadcasted_iota(jnp.int32, stacked, 0) < count * BLK
    wg = wg_ref[hh].reshape(stacked)
    wu = wu_ref[hh].reshape(stacked)
    wg = jnp.where(live_rows, wg, jnp.zeros_like(wg))
    wu = jnp.where(live_rows, wu, jnp.zeros_like(wu))
    wd = jnp.concatenate([wd_ref[hh, p] for p in range(slots)], axis=1)
    live_cols = lax.broadcasted_iota(jnp.int32, wd.shape, 1) < count * BLK
    wd = jnp.where(live_cols, wd, jnp.zeros_like(wd))
    gate = jnp.dot(x, wg, preferred_element_type=f32)
    up = jnp.dot(x, wu, preferred_element_type=f32)
    d_hidden = lax.dot_general(dy, wd, (((1,), (1,)), ((), ())), preferred_element_type=f32)
    sig = 1.0 / (1.0 + jnp.exp(-gate))
    silu = gate * sig
    hidden = (silu * up).astype(jnp.bfloat16)
    d_gate = (d_hidden * up * sig * (1.0 + gate * (1.0 - sig))).astype(jnp.bfloat16)
    d_up = (d_hidden * silu).astype(jnp.bfloat16)
    d_gu = jnp.concatenate([d_gate, d_up], axis=1)
    grad_gu = jnp.dot(x.T, d_gu, preferred_element_type=f32)
    grad_d = jnp.dot(hidden.T, dy, preferred_element_type=f32)
    back_t = jnp.dot(wg, d_gate.T, preferred_element_type=f32)
    back_t = back_t + jnp.dot(wu, d_up.T, preferred_element_type=f32)
    for p in range(slots):
        live = p < count
        zero = jnp.zeros((BLK, BLK), f32)
        rows = slice(p * BLK, (p + 1) * BLK)
        gg_ref[hh, p] = jnp.where(live, grad_gu[rows, :BLK], zero)
        gu_ref[hh, p] = jnp.where(live, grad_gu[rows, BLK:], zero)
        gd_ref[hh, p] = jnp.where(live, grad_d[:, rows], zero)
        dxt_ref[pl.ds(offs[p], BLK), :] += back_t[rows]


def _ffn_kernel(col_ref, cnt_ref, tok_ref, cot_ref, wg_ref, wu_ref, wd_ref,
                gg_ref, gu_ref, gd_ref, dxt_ref):
    step = pl.program_id(0)
    per_step = gg_ref.shape[0]

    @pl.when(step == 0)
    def _():
        dxt_ref[...] = jnp.zeros_like(dxt_ref)

    for hh in range(per_step):
        h = step * per_step + hh
        _ffn_block(hh, h, cnt_ref[h], col_ref, tok_ref, cot_ref, wg_ref, wu_ref, wd_ref,
                   gg_ref, gu_ref, gd_ref, dxt_ref)


def ffn_block_terms(col_index, row_count, full_tok, full_cot, gate_w, up_w, down_w):
    hblk, slots = col_index.shape
    rows, width = full_tok.shape
    per_step = 9 if hblk % 9 == 0 else (3 if hblk % 3 == 0 else 1)
    wspec = pl.BlockSpec((per_step, slots, BLK, BLK), lambda h, c, n: (h, 0, 0, 0))
    full = pl.BlockSpec((rows, width), lambda h, c, n: (0, 0))
    full_t = pl.BlockSpec((width, rows), lambda h, c, n: (0, 0))
    gspec = wspec
    grad = jax.ShapeDtypeStruct((hblk, slots, BLK, BLK), jnp.float32)
    flops = 2 * rows * hblk * slots * BLK * BLK * 9
    return pl.pallas_call(
        _ffn_kernel,
        grid_spec=pltpu.PrefetchScalarGridSpec(
            num_scalar_prefetch=2,
            grid=(hblk // per_step,),
            in_specs=[full, full, wspec, wspec, wspec],
            out_specs=[gspec, gspec, gspec, full_t],
        ),
        out_shape=[grad, grad, grad, jax.ShapeDtypeStruct((width, rows), jnp.float32)],
        compiler_params=pltpu.CompilerParams(dimension_semantics=("arbitrary",)),
        cost_estimate=pl.CostEstimate(
            flops=flops,
            transcendentals=rows * hblk * BLK,
            bytes_accessed=3 * hblk * slots * BLK * BLK * 6 + rows * width * 8,
        ),
        name="ffn_block_terms",
    )(col_index.T, row_count, full_tok, full_cot, gate_w, up_w, down_w)


def shards(n_dp, n_t, tokens, cotangent, w_gate, w_up, w_down, col_index, row_count, adam_m, adam_v):
    swap = [(0, 1), (1, 0)]
    first = lax.axis_index("tensor") == 0
    if n_t == 2:
        other_tok, other_cot = lax.ppermute(jnp.stack([tokens, cotangent]), "tensor", swap)
        full_tok = jnp.concatenate(
            [jnp.where(first, tokens, other_tok), jnp.where(first, other_tok, tokens)], axis=1
        )
        full_cot = jnp.concatenate(
            [jnp.where(first, cotangent, other_cot), jnp.where(first, other_cot, cotangent)], axis=1
        )
    else:
        full_tok = lax.all_gather(tokens, "tensor", axis=1, tiled=True)
        full_cot = lax.all_gather(cotangent, "tensor", axis=1, tiled=True)
    tok_rows = full_tok.shape[0]
    own_rows = w_gate.shape[1] * w_gate.shape[2] * BLK
    grad_gate, grad_up, grad_down, dx_part = ffn_block_terms(
        col_index, row_count, full_tok, full_cot, w_gate[0], w_up[0], w_down[0]
    )
    reduced = jnp.stack(
        ring_reduce_scatter(
            [g.reshape(own_rows, BLK) for g in (grad_gate, grad_up, grad_down)],
            n_dp,
            n_t,
            ring_order(n_dp),
            jnp.bfloat16,
        )
    )[:, None]
    if n_t == 2:
        half = tokens.shape[1]
        lo, hi = dx_part[:half].T, dx_part[half:].T
        mine = jnp.where(first, lo, hi)
        theirs = lax.ppermute(jnp.where(first, hi, lo).astype(jnp.bfloat16), "tensor", swap)
        token_grads = (mine + theirs.astype(jnp.float32)).astype(jnp.bfloat16)
    else:
        token_grads = lax.psum_scatter(
            dx_part.T.astype(jnp.bfloat16), "tensor", scatter_dimension=1, tiled=True
        )
    grad_scale = 1.0 / math.sqrt(n_dp * tok_rows)
    grad_all = reduced * grad_scale
    m_new = 0.9 * adam_m + 0.1 * grad_all
    v_new = 0.95 * adam_v + 0.05 * grad_all * grad_all
    step_dir = m_new / (jnp.sqrt(v_new) + 1e-08)
    return (token_grads, m_new, v_new, step_dir)


def solution(mesh):
    in_specs = (
        P("dp", "tensor"),
        P("dp", "tensor"),
        P("tensor", None, None, None, None),
        P("tensor", None, None, None, None),
        P("tensor", None, None, None, None),
        P("tensor", None),
        P("tensor"),
        P(None, "tensor", "dp", None),
        P(None, "tensor", "dp", None),
    )
    out_specs = (
        P("dp", "tensor"),
        P(None, "tensor", "dp", None),
        P(None, "tensor", "dp", None),
        P(None, "tensor", "dp", None),
    )
    body = functools.partial(shards, mesh.shape["dp"], mesh.shape["tensor"])
    return jax.shard_map(body, mesh=mesh, in_specs=in_specs, out_specs=out_specs, check_vma=False)
```
